512 devices in a mesh: lane: 32 (over y_lo, z, core), rec: 16 (over y_hi, x).
Axes of the slice: x: 4, y: 8 (y_hi: 4, y_lo: 2; y = y_hi * 2 + y_lo), z: 8, core: 2. Of those that a mesh axis runs over, the one named last changes fastest.
Arguments:
- waveforms: bfloat16 [512, 65536], P('lane', 'rec'), may hold values from -6 to 6
- patterns: int32 [512, 65536], P('lane', 'rec'), may hold values from 0 to 3
- partners: int32 [512, 8], P('lane'), may hold values from 0 to 511, as said below
- counts: int32 [512], P('lane'), may hold values from 1 to 8, as said below
Outputs:
- responses: float32 [2, 256, 4096], P(None, 'rec', 'lane')
The draws below stay inside these ranges and needn't reach their ends.
Inputs may be any that keep to these rules, and one draw needn't show every extreme that they name: partners[l, s] is never l; the 8 partners of a lane lie on 8 different indices of lane; of the 128 entries of the lanes of one index of lane, exactly 4 name lanes of each index of lane. `counts`: uneven over lanes and over indices of lane.
All inputs are finite; a program needn't handle non-finite values.
Results may differ from the reference program's by a relative error of at most 0.0003.
Values may be sent and summed in bfloat16 or wider, within the bound.
No kernel may reach another device: no remote copies, remote signals or barrier semaphores. Data moves between devices by JAX's collectives and lax.ppermute only.
A program may use at most 64 MiB of HBM per device.

```python
import jax
import jax.numpy as jnp
from jax import lax

LANE_DEV = 16
SLOTS = 8
LAGS = 256
LANES = 512
TIME = 65536
N_LANE = 32


def draw_partners(key, part):
    key_order, key_local = jax.random.split(jax.random.fold_in(key, 7))
    orders = jax.vmap(lambda single: jax.random.permutation(single, N_LANE))(jax.random.split(key_order, N_LANE))
    serial = jnp.arange(LANE_DEV * SLOTS, dtype=jnp.int32)
    target_dev = orders[:, serial % N_LANE].astype(jnp.int32)
    owner = jnp.arange(N_LANE, dtype=jnp.int32)[:, None]
    own_lane = serial[None, :] // SLOTS
    local = jax.random.randint(key_local, (N_LANE, LANE_DEV * SLOTS), 0, LANE_DEV).astype(jnp.int32)
    local = jnp.where((target_dev == owner) & (local == own_lane), (local + 1) % LANE_DEV, local)
    return (target_dev * LANE_DEV + local).reshape(LANES, SLOTS).astype(jnp.int32)


def draw_counts(key, part):
    key_hot, key_pick, key_count = jax.random.split(jax.random.fold_in(key, 13), 3)
    heavy = jax.random.randint(key_hot, (N_LANE,), 0, 8) == 0
    forced = jax.random.randint(key_pick, (), 0, N_LANE)
    heavy = heavy | (jnp.arange(N_LANE, dtype=jnp.int32) == forced)
    lane_heavy = jnp.repeat(heavy, LANE_DEV)
    light = jax.random.randint(key_count, (LANES,), 1, SLOTS // 2 + 1)
    return jnp.where(lane_heavy, SLOTS, light).astype(jnp.int32)


def set_ends(result, rng, smallest, top_value):
    place = [jax.random.randint(jax.random.fold_in(rng, axis), (), 0, length) for axis, length in enumerate(result.shape)]
    main_axis = result.shape.index(max(result.shape))
    neighbour = place[:main_axis] + [(place[main_axis] + 1) % result.shape[main_axis]] + place[main_axis + 1:]
    return result.at[tuple(place)].set(smallest).at[tuple(neighbour)].set(top_value)


def block_scale(stream_key, dims, cuts, low, top_value):
    gain = 1.0
    for position, parts in cuts:
        draws = jax.random.uniform(jax.random.fold_in(jax.random.fold_in(stream_key, 6), position), (parts,), jnp.float32, low / len(cuts), top_value / len(cuts))
        gain = gain * jnp.repeat(jnp.exp(draws), dims[position] // parts).reshape((-1,) + (1,) * (len(dims) - 1 - position))
    return gain


def noise(rng, shape, width, limit, cuts=(), kind=jnp.bfloat16):
    entries = jax.random.normal(rng, shape, jnp.float32) * width
    if len(cuts) > 0:
        entries = block_scale(rng, shape, cuts, -0.22, 0.18) * entries
    return jnp.clip(entries, min=-limit, max=limit).astype(kind)


def setup_inputs(seed: int = 0) -> dict:
    key_of = jax.random.split(jax.random.key(seed), 5)
    waveforms = noise(key_of[0], (LANES, TIME), 1.0, 6.0, ((0, 32), (1, 16)))
    patterns = set_ends(jax.random.randint(key_of[1], (LANES, TIME), 0, 4), jax.random.fold_in(key_of[1], 1), 0, 3).astype(jnp.int32)
    partners = draw_partners(jax.random.fold_in(key_of[4], 71), 0)
    counts = draw_counts(jax.random.fold_in(key_of[4], 71), 0)
    return {"waveforms": waveforms, "patterns": patterns, "partners": partners, "counts": counts}


def reference(waveforms, patterns, partners, counts):
    length = 2 * TIME
    signal = jnp.fft.rfft(waveforms.astype(jnp.float32), n=length, axis=1)
    levels = (2 * patterns - 3).astype(jnp.float32)
    spectra = jnp.fft.rfft(levels, n=length, axis=1)

    def one_lane(lane):
        chosen = partners[lane]
        forward = jnp.fft.irfft(signal[lane][None, :] * jnp.conj(spectra[chosen]), n=length, axis=1)[:, :LAGS]
        reverse = jnp.fft.irfft(signal[chosen] * jnp.conj(spectra[lane])[None, :], n=length, axis=1)[:, :LAGS]
        return forward, reverse

    forward, reverse = lax.map(one_lane, jnp.arange(LANES, dtype=jnp.int32))
    valid = (jnp.arange(SLOTS, dtype=jnp.int32)[None, :] < counts[:, None]).astype(jnp.float32)
    scale = (5.0 * TIME) ** -0.5
    both = jnp.stack([forward, reverse]) * valid[None, :, :, None] * scale
    both = jnp.transpose(both, (0, 3, 1, 2)).reshape(2, LAGS, LANES * SLOTS)
    return both.astype(jnp.float32)
```

```python
import jax
import jax.numpy as jnp
from jax import lax
from jax.sharding import PartitionSpec as P

LAGS = 256
PHASE = 16


def passed_along(block, axis, distance):
    devices = range(lax.axis_size(axis))
    route = [(i - distance, i) for i in devices if i - distance in devices]
    return lax.ppermute(block, axis, route)


def request_layout(targets, lane_dev, capacity):
    target_dev = targets // lane_dev
    serial = jnp.arange(targets.shape[0], dtype=jnp.int32)
    earlier = (target_dev[None, :] == target_dev[:, None]) & (serial[None, :] < serial[:, None])
    ranks = jnp.sum(earlier.astype(jnp.int32), axis=1)
    slot_of = target_dev * capacity + ranks
    order = jnp.sum(jnp.where(slot_of[None, :] == serial[:, None], serial[None, :], 0), axis=1)
    return (slot_of, order)


def windows(extended, time_dev):
    lanes = extended.shape[0]
    blocks = time_dev // PHASE
    extra = LAGS // PHASE
    phased = extended.reshape(lanes, blocks + extra, PHASE).transpose(0, 2, 1)
    parts = [phased[:, :, q : q + blocks] for q in range(extra + 1)]
    return jnp.stack(parts, axis=1).reshape(lanes, (extra + 1) * PHASE, blocks)


def skew_sum(cross, width):
    total = cross[:, :, 0, 0:width]
    for i in range(1, PHASE):
        total = total + cross[:, :, i, i : i + width]
    return total


def correlate(partner_rows, extended, time_dev):
    lanes, slots, _ = partner_rows.shape
    blocks = time_dev // PHASE
    rows = partner_rows.reshape(lanes, slots, blocks, PHASE).transpose(0, 1, 3, 2)
    win = windows(extended, time_dev)
    cross = jnp.einsum("lsim,ljm->lsij", rows, win, preferred_element_type=jnp.float32)
    return skew_sum(cross, LAGS + 1)


def per_device(waveforms, patterns, partners, counts):
    lane_dev, time_dev = waveforms.shape
    slots = partners.shape[1]
    lane_count = lax.axis_size("lane")
    rec_count = lax.axis_size("rec")
    capacity = lane_dev * slots // lane_count
    total_time = time_dev * rec_count
    levels = (2 * patterns - 3).astype(jnp.bfloat16)
    prev_rim = passed_along(levels[:, time_dev - LAGS :], "rec", 1)
    next_rim = passed_along(waveforms[:, :LAGS], "rec", -1)
    lev_ext = jnp.concatenate([prev_rim, levels], axis=1)
    wav_ext = jnp.concatenate([waveforms, next_rim], axis=1)

    targets = partners.reshape(-1)
    slot_of, order = request_layout(targets, lane_dev, capacity)
    local_index = targets % lane_dev
    send_index = local_index[order].reshape(lane_count, capacity)
    index_in = lax.all_to_all(send_index, "lane", split_axis=0, concat_axis=0, tiled=True)
    both = jnp.stack([waveforms, levels], axis=1)
    reply = both[index_in.reshape(-1)].reshape(lane_count, capacity, 2, time_dev)
    got = lax.all_to_all(reply, "lane", split_axis=0, concat_axis=0, tiled=True)
    mine = got.reshape(lane_count * capacity, 2, time_dev)[slot_of]
    mine = mine.reshape(lane_dev, slots, 2, time_dev)

    forward = correlate(mine[:, :, 1], wav_ext, time_dev)[:, :, :LAGS]
    reverse = correlate(mine[:, :, 0], lev_ext, time_dev)[:, :, LAGS:0:-1]
    terms = jnp.stack([forward, reverse]).reshape(2, lane_dev * slots, LAGS)
    lag_dev = LAGS // rec_count
    terms = terms.reshape(2, lane_dev * slots, rec_count, lag_dev).transpose(2, 0, 3, 1)
    parts = lax.all_to_all(terms, "rec", split_axis=0, concat_axis=0, tiled=True)
    summed = jnp.sum(parts.reshape(rec_count, 2, lag_dev, lane_dev * slots), axis=0)
    valid = (
        (jnp.arange(slots, dtype=jnp.int32)[None, :] < counts[:, None])
        .astype(jnp.float32)
        .reshape(-1)
    )
    scale = (5.0 * total_time) ** (-0.5)
    return summed * valid * scale


def solution(mesh):
    in_specs = (P("lane", "rec"), P("lane", "rec"), P("lane", None), P("lane"))
    out_specs = P(None, "rec", "lane")
    return jax.shard_map(
        per_device, mesh=mesh, in_specs=in_specs, out_specs=out_specs, check_vma=False
    )
```

```python
import jax
import jax.numpy as jnp
from jax import lax
from jax.experimental import pallas as pl
from jax.experimental.pallas import tpu as pltpu
from jax.sharding import PartitionSpec as P

LAGS = 256
PHASE = 16
WIDE = 384


def passed_along(block, axis, distance):
    devices = range(lax.axis_size(axis))
    route = [(i - distance, i) for i in devices if i - distance in devices]
    return lax.ppermute(block, axis, route)


def request_layout(targets, lane_dev, capacity):
    target_dev = targets // lane_dev
    serial = jnp.arange(targets.shape[0], dtype=jnp.int32)
    earlier = (target_dev[None, :] == target_dev[:, None]) & (serial[None, :] < serial[:, None])
    ranks = jnp.sum(earlier.astype(jnp.int32), axis=1)
    slot_of = target_dev * capacity + ranks
    order = jnp.sum(jnp.where(slot_of[None, :] == serial[:, None], serial[None, :], 0), axis=1)
    return (slot_of, order)


def deinterleave(rows):
    lead = rows.shape[:-1]
    n = rows.shape[-1]
    split = rows.reshape(lead + (n // PHASE, PHASE))
    return jnp.swapaxes(split, -1, -2)


def pick_rows(onehot, table):
    flat = table.reshape(table.shape[0], -1)
    out = jnp.dot(onehot, flat, preferred_element_type=jnp.float32).astype(table.dtype)
    return out.reshape((onehot.shape[0],) + table.shape[1:])


def lane_kernel(rows_ref, phased_ref, out_ref, win_ref, cross_ref):
    slots = rows_ref.shape[0]
    blocks = rows_ref.shape[3]
    for d in range(2):
        phased = phased_ref[0, d].astype(jnp.float32)
        for q in range(WIDE // PHASE):
            shifted = phased if q == 0 else pltpu.roll(phased, WIDE - q, 1)
            win_ref[q * PHASE : (q + 1) * PHASE, :] = shifted[:, :blocks].astype(jnp.bfloat16)
        lhs = rows_ref[:, d].reshape(slots * PHASE, blocks)
        cross = lax.dot_general(
            lhs, win_ref[...], (((1,), (1,)), ((), ())), preferred_element_type=jnp.float32
        )
        for c in range(WIDE // 128):
            cross_ref[c] = cross[:, c * 128 : (c + 1) * 128]
        total = None
        for i in range(PHASE):
            picked = jnp.concatenate(
                [cross_ref[c, pl.ds(i, slots, stride=PHASE), :] for c in range(WIDE // 128)], axis=1
            )
            shifted = picked if i == 0 else pltpu.roll(picked, WIDE - i, 1)
            total = shifted[:, :LAGS] if total is None else total + shifted[:, :LAGS]
        out_ref[0, d] = total


def correlate(rows, phased):
    lanes = phased.shape[0]
    slots = rows.shape[0] // lanes
    blocks = rows.shape[3]
    return pl.pallas_call(
        lane_kernel,
        grid=(lanes,),
        in_specs=[
            pl.BlockSpec((slots, 2, PHASE, blocks), lambda l: (l, 0, 0, 0)),
            pl.BlockSpec((1, 2, PHASE, WIDE), lambda l: (l, 0, 0, 0)),
        ],
        out_specs=pl.BlockSpec((1, 2, slots, LAGS), lambda l: (l, 0, 0, 0)),
        out_shape=jax.ShapeDtypeStruct((lanes, 2, slots, LAGS), jnp.float32),
        scratch_shapes=[
            pltpu.VMEM((WIDE, blocks), jnp.bfloat16),
            pltpu.VMEM((WIDE // 128, slots * PHASE, 128), jnp.float32),
        ],
    )(rows, phased)


def per_device(waveforms, patterns, partners, counts):
    lane_dev, time_dev = waveforms.shape
    slots = partners.shape[1]
    lane_count = lax.axis_size("lane")
    rec_count = lax.axis_size("rec")
    capacity = lane_dev * slots // lane_count
    total_time = time_dev * rec_count
    blocks = time_dev // PHASE
    levels = (2 * patterns - 3).astype(jnp.bfloat16)
    prev_rim = passed_along(levels[:, time_dev - LAGS :], "rec", 1)
    next_rim = passed_along(waveforms[:, :LAGS], "rec", -1)
    span = (blocks + WIDE // PHASE) * PHASE
    wav_ext = jnp.concatenate(
        [waveforms, next_rim, jnp.zeros((lane_dev, span - time_dev - LAGS), jnp.bfloat16)], axis=1
    )
    lev_ext = jnp.concatenate(
        [prev_rim[:, 1:], levels, jnp.zeros((lane_dev, span - time_dev - LAGS + 1), jnp.bfloat16)],
        axis=1,
    )
    phased = deinterleave(jnp.stack([wav_ext, lev_ext], axis=1))
    phased = jnp.pad(phased, ((0, 0), (0, 0), (0, 0), (0, WIDE - phased.shape[3])))

    targets = partners.reshape(-1)
    slot_of, order = request_layout(targets, lane_dev, capacity)
    local_index = targets % lane_dev
    send_index = local_index[order].reshape(lane_count, capacity)
    index_in = lax.all_to_all(send_index, "lane", split_axis=0, concat_axis=0, tiled=True)
    both = deinterleave(jnp.stack([waveforms, levels], axis=1))
    pick = (index_in.reshape(-1)[:, None] == jnp.arange(lane_dev)[None, :]).astype(jnp.bfloat16)
    reply = pick_rows(pick, both).reshape((lane_count, capacity) + both.shape[1:])
    got = lax.all_to_all(reply, "lane", split_axis=0, concat_axis=0, tiled=True)
    got = got.reshape((lane_count * capacity,) + both.shape[1:])
    place = (slot_of[:, None] == jnp.arange(lane_count * capacity)[None, :]).astype(jnp.bfloat16)
    mine = pick_rows(place, got)
    mine = jnp.flip(mine, axis=1)

    out = correlate(mine, phased)
    forward = out[:, 0].reshape(lane_dev * slots, LAGS)
    reverse = out[:, 1, :, ::-1].reshape(lane_dev * slots, LAGS)
    terms = jnp.stack([forward, reverse])
    lag_dev = LAGS // rec_count
    terms = terms.reshape(2, lane_dev * slots, rec_count, lag_dev).transpose(2, 0, 3, 1)
    parts = lax.all_to_all(terms, "rec", split_axis=0, concat_axis=0, tiled=True)
    summed = jnp.sum(parts.reshape(rec_count, 2, lag_dev, lane_dev * slots), axis=0)
    valid = (
        (jnp.arange(slots, dtype=jnp.int32)[None, :] < counts[:, None])
        .astype(jnp.float32)
        .reshape(-1)
    )
    scale = (5.0 * total_time) ** (-0.5)
    return summed * valid * scale


def solution(mesh):
    in_specs = (P("lane", "rec"), P("lane", "rec"), P("lane", None), P("lane"))
    out_specs = P(None, "rec", "lane")
    return jax.shard_map(
        per_device, mesh=mesh, in_specs=in_specs, out_specs=out_specs, check_vma=False
    )
```

```python
import jax
import jax.numpy as jnp
from jax import lax
from jax.experimental import pallas as pl
from jax.experimental.pallas import tpu as pltpu
from jax.sharding import PartitionSpec as P

LAGS = 256
PHASE = 16
WIDE = 384


def passed_along(block, axis, distance):
    devices = range(lax.axis_size(axis))
    route = [(i - distance, i) for i in devices if i - distance in devices]
    return lax.ppermute(block, axis, route)


def request_layout(targets, lane_dev, capacity):
    target_dev = targets // lane_dev
    serial = jnp.arange(targets.shape[0], dtype=jnp.int32)
    earlier = (target_dev[None, :] == target_dev[:, None]) & (serial[None, :] < serial[:, None])
    ranks = jnp.sum(earlier.astype(jnp.int32), axis=1)
    slot_of = target_dev * capacity + ranks
    order = jnp.sum(jnp.where(slot_of[None, :] == serial[:, None], serial[None, :], 0), axis=1)
    return (slot_of, order)


def deinterleave(rows):
    lead = rows.shape[:-1]
    n = rows.shape[-1]
    split = rows.reshape(lead + (n // PHASE, PHASE))
    return jnp.swapaxes(split, -1, -2)


def pick_rows(onehot, table):
    flat = table.reshape(table.shape[0], -1)
    out = jnp.dot(onehot, flat, preferred_element_type=jnp.float32).astype(table.dtype)
    return out.reshape((onehot.shape[0],) + table.shape[1:])


def lane_kernel(slot_ref, *refs):
    del slot_ref
    acc_ref = refs[-1]
    cross_ref = refs[-2]
    win_ref = refs[-3]
    out_ref = refs[-4]
    phased_ref = refs[-5]
    row_refs = refs[:-5]
    slots = len(row_refs)
    blocks = win_ref.shape[1]
    top = WIDE // PHASE - 1
    lane = pl.program_id(0)
    for d in range(2):
        phased = phased_ref[0, d].astype(jnp.float32)
        for q in range(WIDE // PHASE):
            step = q if d == 0 else top - q
            shifted = phased if step == 0 else pltpu.roll(phased, WIDE - step, 1)
            win_ref[q * PHASE : (q + 1) * PHASE, :] = shifted[:, :blocks].astype(jnp.bfloat16)
        lhs = jnp.concatenate([ref[0, 1 - d] for ref in row_refs], axis=0)
        cross = lax.dot_general(
            lhs, win_ref[...], (((1,), (1,)), ((), ())), preferred_element_type=jnp.float32
        )
        for c in range(WIDE // 128):
            cross_ref[c] = cross[:, c * 128 : (c + 1) * 128]
        total = None
        for i in range(PHASE):
            picked = jnp.concatenate(
                [cross_ref[c, pl.ds(i, slots, stride=PHASE), :] for c in range(WIDE // 128)], axis=1
            )
            step = i if d == 0 else (WIDE - LAGS) - i
            shifted = picked if step == 0 else pltpu.roll(picked, WIDE - step, 1)
            total = shifted[:, :LAGS] if total is None else total + shifted[:, :LAGS]
        acc_ref[d, pl.ds(pl.multiple_of(lane * slots, slots), slots), :] = total

    @pl.when(lane == pl.num_programs(0) - 1)
    def _():
        for d in range(2):
            flipped = acc_ref[d].T
            out_ref[:, d] = flipped.reshape(out_ref.shape[0], out_ref.shape[2], out_ref.shape[3])


def correlate(got, slot_of, phased, rec_count):
    lanes = phased.shape[0]
    pairs = slot_of.shape[0]
    slots = pairs // lanes
    blocks = got.shape[3]
    lag_dev = LAGS // rec_count

    def row_spec(s):
        return pl.BlockSpec((1, 2, PHASE, blocks), lambda l, slot: (slot[l * slots + s], 0, 0, 0))

    grid_spec = pltpu.PrefetchScalarGridSpec(
        num_scalar_prefetch=1,
        grid=(lanes,),
        in_specs=[row_spec(s) for s in range(slots)]
        + [pl.BlockSpec((1, 2, PHASE, WIDE), lambda l, slot: (l, 0, 0, 0))],
        out_specs=pl.BlockSpec((rec_count, 2, lag_dev, pairs), lambda l, slot: (0, 0, 0, 0)),
        scratch_shapes=[
            pltpu.VMEM((WIDE, blocks), jnp.bfloat16),
            pltpu.VMEM((WIDE // 128, slots * PHASE, 128), jnp.float32),
            pltpu.VMEM((2, pairs, LAGS), jnp.float32),
        ],
    )
    return pl.pallas_call(
        lane_kernel,
        grid_spec=grid_spec,
        out_shape=jax.ShapeDtypeStruct((rec_count, 2, lag_dev, pairs), jnp.float32),
    )(slot_of, *([got] * slots), phased)


def per_device(waveforms, patterns, partners, counts):
    lane_dev, time_dev = waveforms.shape
    slots = partners.shape[1]
    lane_count = lax.axis_size("lane")
    rec_count = lax.axis_size("rec")
    capacity = lane_dev * slots // lane_count
    total_time = time_dev * rec_count
    blocks = time_dev // PHASE
    levels = (2 * patterns - 3).astype(jnp.bfloat16)
    prev_rim = passed_along(levels[:, time_dev - LAGS :], "rec", 1)
    next_rim = passed_along(waveforms[:, :LAGS], "rec", -1)
    span = (blocks + WIDE // PHASE) * PHASE
    wav_ext = jnp.concatenate(
        [waveforms, next_rim, jnp.zeros((lane_dev, span - time_dev - LAGS), jnp.bfloat16)], axis=1
    )
    lev_ext = jnp.concatenate(
        [prev_rim[:, 1:], levels, jnp.zeros((lane_dev, span - time_dev - LAGS + 1), jnp.bfloat16)],
        axis=1,
    )
    phased = deinterleave(jnp.stack([wav_ext, lev_ext], axis=1))
    phased = jnp.concatenate([phased[:, :1], phased[:, 1:, ::-1]], axis=1)
    phased = jnp.pad(phased, ((0, 0), (0, 0), (0, 0), (0, WIDE - phased.shape[3])))

    targets = partners.reshape(-1)
    slot_of, order = request_layout(targets, lane_dev, capacity)
    local_index = targets % lane_dev
    send_index = local_index[order].reshape(lane_count, capacity)
    index_in = lax.all_to_all(send_index, "lane", split_axis=0, concat_axis=0, tiled=True)
    both = deinterleave(jnp.stack([waveforms, levels], axis=1))
    pick = (index_in.reshape(-1)[:, None] == jnp.arange(lane_dev)[None, :]).astype(jnp.bfloat16)
    reply = pick_rows(pick, both).reshape((lane_count, capacity) + both.shape[1:])
    got = lax.all_to_all(reply, "lane", split_axis=0, concat_axis=0, tiled=True)
    got = got.reshape((lane_count * capacity,) + both.shape[1:])
    lag_dev = LAGS // rec_count
    terms = correlate(got, slot_of, phased, rec_count)
    parts = lax.all_to_all(terms, "rec", split_axis=0, concat_axis=0, tiled=True)
    summed = jnp.sum(parts.reshape(rec_count, 2, lag_dev, lane_dev * slots), axis=0)
    valid = (
        (jnp.arange(slots, dtype=jnp.int32)[None, :] < counts[:, None])
        .astype(jnp.float32)
        .reshape(-1)
    )
    scale = (5.0 * total_time) ** (-0.5)
    return summed * valid * scale


def solution(mesh):
    in_specs = (P("lane", "rec"), P("lane", "rec"), P("lane", None), P("lane"))
    out_specs = P(None, "rec", "lane")
    return jax.shard_map(
        per_device, mesh=mesh, in_specs=in_specs, out_specs=out_specs, check_vma=False
    )
```

```python
import jax
import jax.numpy as jnp
from jax import lax
from jax.experimental import pallas as pl
from jax.experimental.pallas import tpu as pltpu
from jax.sharding import PartitionSpec as P

LAGS = 256
PHASE = 16
WIDE = 384


def passed_along(block, axis, distance):
    devices = range(lax.axis_size(axis))
    route = [(i - distance, i) for i in devices if i - distance in devices]
    return lax.ppermute(block, axis, route)


def request_layout(targets, lane_dev, capacity):
    target_dev = targets // lane_dev
    serial = jnp.arange(targets.shape[0], dtype=jnp.int32)
    earlier = (target_dev[None, :] == target_dev[:, None]) & (serial[None, :] < serial[:, None])
    ranks = jnp.sum(earlier.astype(jnp.int32), axis=1)
    slot_of = target_dev * capacity + ranks
    order = jnp.sum(jnp.where(slot_of[None, :] == serial[:, None], serial[None, :], 0), axis=1)
    return (slot_of, order)


def deinterleave(rows):
    lead = rows.shape[:-1]
    n = rows.shape[-1]
    split = rows.reshape(lead + (n // PHASE, PHASE))
    return jnp.swapaxes(split, -1, -2)


def pick_rows(onehot, table):
    flat = table.reshape(table.shape[0], -1)
    out = jnp.dot(onehot, flat, preferred_element_type=jnp.float32).astype(table.dtype)
    return out.reshape((onehot.shape[0],) + table.shape[1:])


def window_kernel(phased_ref, win_ref):
    blocks = win_ref.shape[3]
    top = WIDE // PHASE - 1
    for d in range(2):
        phased = phased_ref[0, d].astype(jnp.float32)
        for q in range(WIDE // PHASE):
            step = q if d == 0 else top - q
            shifted = phased if step == 0 else pltpu.roll(phased, WIDE - step, 1)
            win_ref[0, d, q * PHASE : (q + 1) * PHASE, :] = shifted[:, :blocks].astype(jnp.bfloat16)


def windows(phased, blocks):
    lanes = phased.shape[0]
    return pl.pallas_call(
        window_kernel,
        grid=(lanes,),
        in_specs=[pl.BlockSpec((1, 2, PHASE, WIDE), lambda l: (l, 0, 0, 0))],
        out_specs=pl.BlockSpec((1, 2, WIDE, blocks), lambda l: (l, 0, 0, 0)),
        out_shape=jax.ShapeDtypeStruct((lanes, 2, WIDE, blocks), jnp.bfloat16),
    )(phased)


def lane_kernel(slot_ref, *refs):
    del slot_ref
    acc_ref = refs[-1]
    cross_ref = refs[-2]
    out_ref = refs[-3]
    win_ref = refs[-4]
    row_refs = refs[:-4]
    slots = len(row_refs)
    lane = pl.program_id(0)
    for d in range(2):
        lhs = jnp.concatenate([ref[0, 1 - d] for ref in row_refs], axis=0)
        cross = lax.dot_general(
            lhs, win_ref[0, d], (((1,), (1,)), ((), ())), preferred_element_type=jnp.float32
        )
        for c in range(WIDE // 128):
            cross_ref[c] = cross[:, c * 128 : (c + 1) * 128]
        total = None
        for i in range(PHASE):
            picked = jnp.concatenate(
                [cross_ref[c, pl.ds(i, slots, stride=PHASE), :] for c in range(WIDE // 128)], axis=1
            )
            step = i if d == 0 else (WIDE - LAGS) - i
            shifted = picked if step == 0 else pltpu.roll(picked, WIDE - step, 1)
            total = shifted[:, :LAGS] if total is None else total + shifted[:, :LAGS]
        acc_ref[d, pl.ds(pl.multiple_of(lane * slots, slots), slots), :] = total

    @pl.when(lane == pl.num_programs(0) - 1)
    def _():
        for d in range(2):
            flipped = acc_ref[d].T
            out_ref[:, d] = flipped.reshape(out_ref.shape[0], out_ref.shape[2], out_ref.shape[3])


def correlate(got, slot_of, wins, rec_count):
    lanes = wins.shape[0]
    pairs = slot_of.shape[0]
    slots = pairs // lanes
    blocks = got.shape[3]
    lag_dev = LAGS // rec_count

    def row_spec(s):
        return pl.BlockSpec((1, 2, PHASE, blocks), lambda l, slot: (slot[l * slots + s], 0, 0, 0))

    grid_spec = pltpu.PrefetchScalarGridSpec(
        num_scalar_prefetch=1,
        grid=(lanes,),
        in_specs=[row_spec(s) for s in range(slots)]
        + [pl.BlockSpec((1, 2, WIDE, blocks), lambda l, slot: (l, 0, 0, 0))],
        out_specs=pl.BlockSpec((rec_count, 2, lag_dev, pairs), lambda l, slot: (0, 0, 0, 0)),
        scratch_shapes=[
            pltpu.VMEM((WIDE // 128, slots * PHASE, 128), jnp.float32),
            pltpu.VMEM((2, pairs, LAGS), jnp.float32),
        ],
    )
    return pl.pallas_call(
        lane_kernel,
        grid_spec=grid_spec,
        out_shape=jax.ShapeDtypeStruct((rec_count, 2, lag_dev, pairs), jnp.float32),
    )(slot_of, *([got] * slots), wins)


def per_device(waveforms, patterns, partners, counts):
    lane_dev, time_dev = waveforms.shape
    slots = partners.shape[1]
    lane_count = lax.axis_size("lane")
    rec_count = lax.axis_size("rec")
    capacity = lane_dev * slots // lane_count
    total_time = time_dev * rec_count
    blocks = time_dev // PHASE
    levels = (2 * patterns - 3).astype(jnp.bfloat16)
    prev_rim = passed_along(levels[:, time_dev - LAGS :], "rec", 1)
    next_rim = passed_along(waveforms[:, :LAGS], "rec", -1)
    span = (blocks + WIDE // PHASE) * PHASE
    wav_ext = jnp.concatenate(
        [waveforms, next_rim, jnp.zeros((lane_dev, span - time_dev - LAGS), jnp.bfloat16)], axis=1
    )
    lev_ext = jnp.concatenate(
        [prev_rim[:, 1:], levels, jnp.zeros((lane_dev, span - time_dev - LAGS + 1), jnp.bfloat16)],
        axis=1,
    )
    phased = deinterleave(jnp.stack([wav_ext, lev_ext], axis=1))
    phased = jnp.concatenate([phased[:, :1], phased[:, 1:, ::-1]], axis=1)
    phased = jnp.pad(phased, ((0, 0), (0, 0), (0, 0), (0, WIDE - phased.shape[3])))

    targets = partners.reshape(-1)
    slot_of, order = request_layout(targets, lane_dev, capacity)
    local_index = targets % lane_dev
    send_index = local_index[order].reshape(lane_count, capacity)
    index_in = lax.all_to_all(send_index, "lane", split_axis=0, concat_axis=0, tiled=True)
    both = deinterleave(jnp.stack([waveforms, levels], axis=1))
    pick = (index_in.reshape(-1)[:, None] == jnp.arange(lane_dev)[None, :]).astype(jnp.bfloat16)
    reply = pick_rows(pick, both).reshape((lane_count, capacity) + both.shape[1:])
    got = lax.all_to_all(reply, "lane", split_axis=0, concat_axis=0, tiled=True)
    got = got.reshape((lane_count * capacity,) + both.shape[1:])
    lag_dev = LAGS // rec_count
    terms = correlate(got, slot_of, windows(phased, blocks), rec_count)
    parts = lax.all_to_all(terms, "rec", split_axis=0, concat_axis=0, tiled=True)
    summed = jnp.sum(parts.reshape(rec_count, 2, lag_dev, lane_dev * slots), axis=0)
    valid = (
        (jnp.arange(slots, dtype=jnp.int32)[None, :] < counts[:, None])
        .astype(jnp.float32)
        .reshape(-1)
    )
    scale = (5.0 * total_time) ** (-0.5)
    return summed * valid * scale


def solution(mesh):
    in_specs = (P("lane", "rec"), P("lane", "rec"), P("lane", None), P("lane"))
    out_specs = P(None, "rec", "lane")
    return jax.shard_map(
        per_device, mesh=mesh, in_specs=in_specs, out_specs=out_specs, check_vma=False
    )
```

```python
import jax
import jax.numpy as jnp
from jax import lax
from jax.experimental import pallas as pl
from jax.experimental.pallas import tpu as pltpu
from jax.sharding import PartitionSpec as P

LAGS = 256
PHASE = 16
WIDE = 384


def passed_along(block, axis, distance):
    devices = range(lax.axis_size(axis))
    route = [(i - distance, i) for i in devices if i - distance in devices]
    return lax.ppermute(block, axis, route)


def request_layout(targets, lane_dev, capacity):
    target_dev = targets // lane_dev
    serial = jnp.arange(targets.shape[0], dtype=jnp.int32)
    earlier = (target_dev[None, :] == target_dev[:, None]) & (serial[None, :] < serial[:, None])
    ranks = jnp.sum(earlier.astype(jnp.int32), axis=1)
    slot_of = target_dev * capacity + ranks
    order = jnp.sum(jnp.where(slot_of[None, :] == serial[:, None], serial[None, :], 0), axis=1)
    return (slot_of, order)


def deinterleave(rows):
    lead = rows.shape[:-1]
    n = rows.shape[-1]
    split = rows.reshape(lead + (n // PHASE, PHASE))
    return jnp.swapaxes(split, -1, -2)


def pick_rows(onehot, table):
    flat = table.reshape(table.shape[0], -1)
    out = jnp.dot(onehot, flat, preferred_element_type=jnp.float32).astype(table.dtype)
    return out.reshape((onehot.shape[0],) + table.shape[1:])


def window_kernel(phased_ref, win_ref):
    blocks = win_ref.shape[2]
    top = WIDE // PHASE - 1
    for d in range(2):
        phased = phased_ref[0, d].astype(jnp.float32)
        parts = []
        for q in range(WIDE // PHASE):
            step = q if d == 0 else top - q
            shifted = phased if step == 0 else pltpu.roll(phased, WIDE - step, 1)
            parts.append(shifted[:, :blocks])
        win_ref[0, d] = jnp.concatenate(parts, axis=0).T.astype(jnp.bfloat16)


def windows(phased, blocks):
    lanes = phased.shape[0]
    return pl.pallas_call(
        window_kernel,
        grid=(lanes,),
        in_specs=[pl.BlockSpec((1, 2, PHASE, WIDE), lambda l: (l, 0, 0, 0))],
        out_specs=pl.BlockSpec((1, 2, blocks, WIDE), lambda l: (l, 0, 0, 0)),
        out_shape=jax.ShapeDtypeStruct((lanes, 2, blocks, WIDE), jnp.bfloat16),
    )(phased)


def lane_kernel(slot_ref, *refs):
    del slot_ref
    acc_ref = refs[-1]
    cross_ref = refs[-2]
    out_ref = refs[-3]
    win_ref = refs[-4]
    row_refs = refs[:-4]
    slots = len(row_refs)
    lane = pl.program_id(0)
    for d in range(2):
        lhs = jnp.concatenate([ref[0, 1 - d] for ref in row_refs], axis=0)
        cross = lax.dot_general(
            lhs, win_ref[0, d], (((1,), (0,)), ((), ())), preferred_element_type=jnp.float32
        )
        for c in range(WIDE // 128):
            cross_ref[c] = cross[:, c * 128 : (c + 1) * 128]
        total = None
        for i in range(PHASE):
            picked = jnp.concatenate(
                [cross_ref[c, pl.ds(i, slots, stride=PHASE), :] for c in range(WIDE // 128)], axis=1
            )
            step = i if d == 0 else (WIDE - LAGS) - i
            shifted = picked if step == 0 else pltpu.roll(picked, WIDE - step, 1)
            total = shifted[:, :LAGS] if total is None else total + shifted[:, :LAGS]
        acc_ref[d, pl.ds(pl.multiple_of(lane * slots, slots), slots), :] = total

    @pl.when(lane == pl.num_programs(0) - 1)
    def _():
        for d in range(2):
            flipped = acc_ref[d].T
            out_ref[:, d] = flipped.reshape(out_ref.shape[0], out_ref.shape[2], out_ref.shape[3])


def correlate(got, slot_of, wins, rec_count):
    lanes = wins.shape[0]
    pairs = slot_of.shape[0]
    slots = pairs // lanes
    blocks = got.shape[3]
    lag_dev = LAGS // rec_count

    def row_spec(s):
        return pl.BlockSpec((1, 2, PHASE, blocks), lambda l, slot: (slot[l * slots + s], 0, 0, 0))

    grid_spec = pltpu.PrefetchScalarGridSpec(
        num_scalar_prefetch=1,
        grid=(lanes,),
        in_specs=[row_spec(s) for s in range(slots)]
        + [pl.BlockSpec((1, 2, blocks, WIDE), lambda l, slot: (l, 0, 0, 0))],
        out_specs=pl.BlockSpec((rec_count, 2, lag_dev, pairs), lambda l, slot: (0, 0, 0, 0)),
        scratch_shapes=[
            pltpu.VMEM((WIDE // 128, slots * PHASE, 128), jnp.float32),
            pltpu.VMEM((2, pairs, LAGS), jnp.float32),
        ],
    )
    return pl.pallas_call(
        lane_kernel,
        grid_spec=grid_spec,
        out_shape=jax.ShapeDtypeStruct((rec_count, 2, lag_dev, pairs), jnp.float32),
    )(slot_of, *([got] * slots), wins)


def per_device(waveforms, patterns, partners, counts):
    lane_dev, time_dev = waveforms.shape
    slots = partners.shape[1]
    lane_count = lax.axis_size("lane")
    rec_count = lax.axis_size("rec")
    capacity = lane_dev * slots // lane_count
    total_time = time_dev * rec_count
    blocks = time_dev // PHASE
    levels = (2 * patterns - 3).astype(jnp.bfloat16)
    prev_rim = passed_along(levels[:, time_dev - LAGS :], "rec", 1)
    next_rim = passed_along(waveforms[:, :LAGS], "rec", -1)
    span = (blocks + WIDE // PHASE) * PHASE
    wav_ext = jnp.concatenate(
        [waveforms, next_rim, jnp.zeros((lane_dev, span - time_dev - LAGS), jnp.bfloat16)], axis=1
    )
    lev_ext = jnp.concatenate(
        [prev_rim[:, 1:], levels, jnp.zeros((lane_dev, span - time_dev - LAGS + 1), jnp.bfloat16)],
        axis=1,
    )
    phased = deinterleave(jnp.stack([wav_ext, lev_ext], axis=1))
    phased = jnp.concatenate([phased[:, :1], phased[:, 1:, ::-1]], axis=1)
    phased = jnp.pad(phased, ((0, 0), (0, 0), (0, 0), (0, WIDE - phased.shape[3])))

    targets = partners.reshape(-1)
    slot_of, order = request_layout(targets, lane_dev, capacity)
    local_index = targets % lane_dev
    send_index = local_index[order].reshape(lane_count, capacity)
    index_in = lax.all_to_all(send_index, "lane", split_axis=0, concat_axis=0, tiled=True)
    both = deinterleave(jnp.stack([waveforms, levels], axis=1))
    pick = (index_in.reshape(-1)[:, None] == jnp.arange(lane_dev)[None, :]).astype(jnp.bfloat16)
    reply = pick_rows(pick, both).reshape((lane_count, capacity) + both.shape[1:])
    got = lax.all_to_all(reply, "lane", split_axis=0, concat_axis=0, tiled=True)
    got = got.reshape((lane_count * capacity,) + both.shape[1:])
    lag_dev = LAGS // rec_count
    terms = correlate(got, slot_of, windows(phased, blocks), rec_count)
    parts = lax.all_to_all(terms, "rec", split_axis=0, concat_axis=0, tiled=True)
    summed = jnp.sum(parts.reshape(rec_count, 2, lag_dev, lane_dev * slots), axis=0)
    valid = (
        (jnp.arange(slots, dtype=jnp.int32)[None, :] < counts[:, None])
        .astype(jnp.float32)
        .reshape(-1)
    )
    scale = (5.0 * total_time) ** (-0.5)
    return summed * valid * scale


def solution(mesh):
    in_specs = (P("lane", "rec"), P("lane", "rec"), P("lane", None), P("lane"))
    out_specs = P(None, "rec", "lane")
    return jax.shard_map(
        per_device, mesh=mesh, in_specs=in_specs, out_specs=out_specs, check_vma=False
    )
```

```python
import jax
import jax.numpy as jnp
from jax import lax
from jax.experimental import pallas as pl
from jax.experimental.pallas import tpu as pltpu
from jax.sharding import PartitionSpec as P

LAGS = 256
PHASE = 16
WIDE = 384


def passed_along(block, axis, distance):
    devices = range(lax.axis_size(axis))
    route = [(i - distance, i) for i in devices if i - distance in devices]
    return lax.ppermute(block, axis, route)


def request_layout(targets, lane_dev, capacity):
    target_dev = targets // lane_dev
    serial = jnp.arange(targets.shape[0], dtype=jnp.int32)
    earlier = (target_dev[None, :] == target_dev[:, None]) & (serial[None, :] < serial[:, None])
    ranks = jnp.sum(earlier.astype(jnp.int32), axis=1)
    slot_of = target_dev * capacity + ranks
    order = jnp.sum(jnp.where(slot_of[None, :] == serial[:, None], serial[None, :], 0), axis=1)
    return (slot_of, order)


def deinterleave(rows):
    lead = rows.shape[:-1]
    n = rows.shape[-1]
    split = rows.reshape(lead + (n // PHASE, PHASE))
    return jnp.swapaxes(split, -1, -2)


def pick_rows(onehot, table):
    flat = table.reshape(table.shape[0], -1)
    out = jnp.dot(onehot, flat, preferred_element_type=jnp.float32).astype(table.dtype)
    return out.reshape((onehot.shape[0],) + table.shape[1:])


def window_kernel(phased_ref, win_ref):
    blocks = win_ref.shape[2]
    top = WIDE // PHASE - 1
    for d in range(2):
        phased = phased_ref[0, d].astype(jnp.float32)
        parts = []
        for q in range(WIDE // PHASE):
            step = q if d == 0 else top - q
            shifted = phased if step == 0 else pltpu.roll(phased, WIDE - step, 1)
            parts.append(shifted[:, :blocks])
        win_ref[0, d] = jnp.concatenate(parts, axis=0).T.astype(jnp.bfloat16)


def windows(phased, blocks):
    lanes = phased.shape[0]
    return pl.pallas_call(
        window_kernel,
        grid=(lanes,),
        in_specs=[pl.BlockSpec((1, 2, PHASE, WIDE), lambda l: (l, 0, 0, 0))],
        out_specs=pl.BlockSpec((1, 2, blocks, WIDE), lambda l: (l, 0, 0, 0)),
        out_shape=jax.ShapeDtypeStruct((lanes, 2, blocks, WIDE), jnp.bfloat16),
    )(phased)


def lane_kernel(slot_ref, *refs):
    del slot_ref
    acc_ref = refs[-1]
    out_ref = refs[-2]
    win_ref = refs[-3]
    row_refs = refs[:-3]
    slots = len(row_refs)
    lane = pl.program_id(0)
    for d in range(2):
        lhs = jnp.concatenate([ref[0, 1 - d] for ref in row_refs], axis=0)
        cross = lax.dot_general(
            lhs, win_ref[0, d], (((1,), (0,)), ((), ())), preferred_element_type=jnp.float32
        )
        base = WIDE - (PHASE - 1) if d == 0 else LAGS
        sums = []
        for s in range(slots):
            block = cross[s * PHASE : (s + 1) * PHASE, :]
            lined = pltpu.roll(block, base, 1, stride=1, stride_axis=0)
            sums.append(jnp.sum(lined, axis=0, keepdims=True))
        total = jnp.concatenate(sums, axis=0)[:, :LAGS]
        acc_ref[d, pl.ds(pl.multiple_of(lane * slots, slots), slots), :] = total

    @pl.when(lane == pl.num_programs(0) - 1)
    def _():
        for d in range(2):
            flipped = acc_ref[d].T
            out_ref[:, d] = flipped.reshape(out_ref.shape[0], out_ref.shape[2], out_ref.shape[3])


def correlate(got, slot_of, wins, rec_count):
    lanes = wins.shape[0]
    pairs = slot_of.shape[0]
    slots = pairs // lanes
    blocks = got.shape[3]
    lag_dev = LAGS // rec_count

    def row_spec(s):
        return pl.BlockSpec((1, 2, PHASE, blocks), lambda l, slot: (slot[l * slots + s], 0, 0, 0))

    grid_spec = pltpu.PrefetchScalarGridSpec(
        num_scalar_prefetch=1,
        grid=(lanes,),
        in_specs=[row_spec(s) for s in range(slots)]
        + [pl.BlockSpec((1, 2, blocks, WIDE), lambda l, slot: (l, 0, 0, 0))],
        out_specs=pl.BlockSpec((rec_count, 2, lag_dev, pairs), lambda l, slot: (0, 0, 0, 0)),
        scratch_shapes=[
            pltpu.VMEM((2, pairs, LAGS), jnp.float32),
        ],
    )
    return pl.pallas_call(
        lane_kernel,
        grid_spec=grid_spec,
        out_shape=jax.ShapeDtypeStruct((rec_count, 2, lag_dev, pairs), jnp.float32),
    )(slot_of, *([got] * slots), wins)


def per_device(waveforms, patterns, partners, counts):
    lane_dev, time_dev = waveforms.shape
    slots = partners.shape[1]
    lane_count = lax.axis_size("lane")
    rec_count = lax.axis_size("rec")
    capacity = lane_dev * slots // lane_count
    total_time = time_dev * rec_count
    blocks = time_dev // PHASE
    levels = (2 * patterns - 3).astype(jnp.bfloat16)
    prev_rim = passed_along(levels[:, time_dev - LAGS :], "rec", 1)
    next_rim = passed_along(waveforms[:, :LAGS], "rec", -1)
    span = (blocks + WIDE // PHASE) * PHASE
    wav_ext = jnp.concatenate(
        [waveforms, next_rim, jnp.zeros((lane_dev, span - time_dev - LAGS), jnp.bfloat16)], axis=1
    )
    lev_ext = jnp.concatenate(
        [prev_rim[:, 1:], levels, jnp.zeros((lane_dev, span - time_dev - LAGS + 1), jnp.bfloat16)],
        axis=1,
    )
    phased = deinterleave(jnp.stack([wav_ext, lev_ext], axis=1))
    phased = jnp.concatenate([phased[:, :1], phased[:, 1:, ::-1]], axis=1)
    phased = jnp.pad(phased, ((0, 0), (0, 0), (0, 0), (0, WIDE - phased.shape[3])))

    targets = partners.reshape(-1)
    slot_of, order = request_layout(targets, lane_dev, capacity)
    local_index = targets % lane_dev
    send_index = local_index[order].reshape(lane_count, capacity)
    index_in = lax.all_to_all(send_index, "lane", split_axis=0, concat_axis=0, tiled=True)
    both = deinterleave(jnp.stack([waveforms, levels], axis=1))
    both = jnp.concatenate([both[:, :1], both[:, 1:, ::-1]], axis=1)
    pick = (index_in.reshape(-1)[:, None] == jnp.arange(lane_dev)[None, :]).astype(jnp.bfloat16)
    reply = pick_rows(pick, both).reshape((lane_count, capacity) + both.shape[1:])
    got = lax.all_to_all(reply, "lane", split_axis=0, concat_axis=0, tiled=True)
    got = got.reshape((lane_count * capacity,) + both.shape[1:])
    lag_dev = LAGS // rec_count
    terms = correlate(got, slot_of, windows(phased, blocks), rec_count)
    parts = lax.all_to_all(terms, "rec", split_axis=0, concat_axis=0, tiled=True)
    summed = jnp.sum(parts.reshape(rec_count, 2, lag_dev, lane_dev * slots), axis=0)
    valid = (
        (jnp.arange(slots, dtype=jnp.int32)[None, :] < counts[:, None])
        .astype(jnp.float32)
        .reshape(-1)
    )
    scale = (5.0 * total_time) ** (-0.5)
    return summed * valid * scale


def solution(mesh):
    in_specs = (P("lane", "rec"), P("lane", "rec"), P("lane", None), P("lane"))
    out_specs = P(None, "rec", "lane")
    return jax.shard_map(
        per_device, mesh=mesh, in_specs=in_specs, out_specs=out_specs, check_vma=False
    )
```

```python
import functools

import jax
import jax.numpy as jnp
from jax import lax
from jax.experimental import pallas as pl
from jax.experimental.pallas import tpu as pltpu
from jax.sharding import PartitionSpec as P

LAGS = 256
PHASE = 16
WIDE = 384


def passed_along(block, axis, distance):
    devices = range(lax.axis_size(axis))
    route = [(i - distance, i) for i in devices if i - distance in devices]
    return lax.ppermute(block, axis, route)


def request_layout(targets, lane_dev, capacity):
    target_dev = targets // lane_dev
    serial = jnp.arange(targets.shape[0], dtype=jnp.int32)
    earlier = (target_dev[None, :] == target_dev[:, None]) & (serial[None, :] < serial[:, None])
    ranks = jnp.sum(earlier.astype(jnp.int32), axis=1)
    slot_of = target_dev * capacity + ranks
    order = jnp.sum(jnp.where(slot_of[None, :] == serial[:, None], serial[None, :], 0), axis=1)
    return (slot_of, order)


def deinterleave(rows):
    lead = rows.shape[:-1]
    n = rows.shape[-1]
    split = rows.reshape(lead + (n // PHASE, PHASE))
    return jnp.swapaxes(split, -1, -2)


def pick_rows(onehot, table):
    flat = table.reshape(table.shape[0], -1)
    out = jnp.dot(onehot, flat, preferred_element_type=jnp.float32).astype(table.dtype)
    return out.reshape((onehot.shape[0],) + table.shape[1:])


def window_kernel(phased_ref, win_ref):
    blocks = win_ref.shape[2]
    top = WIDE // PHASE - 1
    for d in range(2):
        phased = phased_ref[0, d].astype(jnp.float32)
        parts = []
        for q in range(WIDE // PHASE):
            step = q if d == 0 else top - q
            shifted = phased if step == 0 else pltpu.roll(phased, WIDE - step, 1)
            parts.append(shifted[:, :blocks])
        win_ref[0, d] = jnp.concatenate(parts, axis=0).T.astype(jnp.bfloat16)


def windows(phased, blocks):
    lanes = phased.shape[0]
    return pl.pallas_call(
        window_kernel,
        grid=(lanes,),
        in_specs=[pl.BlockSpec((1, 2, PHASE, WIDE), lambda l: (l, 0, 0, 0))],
        out_specs=pl.BlockSpec((1, 2, blocks, WIDE), lambda l: (l, 0, 0, 0)),
        out_shape=jax.ShapeDtypeStruct((lanes, 2, blocks, WIDE), jnp.bfloat16),
    )(phased)


def lane_kernel(slots, slot_ref, got_ref, win_ref, out_ref, acc_ref):
    lane = pl.program_id(0)
    for d in range(2):
        lhs = jnp.concatenate(
            [got_ref[slot_ref[lane * slots + s], 1 - d] for s in range(slots)], axis=0
        )
        cross = lax.dot_general(
            lhs, win_ref[0, d], (((1,), (0,)), ((), ())), preferred_element_type=jnp.float32
        )
        base = WIDE - (PHASE - 1) if d == 0 else LAGS
        sums = []
        for s in range(slots):
            block = cross[s * PHASE : (s + 1) * PHASE, :]
            lined = pltpu.roll(block, base, 1, stride=1, stride_axis=0)
            sums.append(jnp.sum(lined, axis=0, keepdims=True))
        total = jnp.concatenate(sums, axis=0)[:, :LAGS]
        acc_ref[d, pl.ds(pl.multiple_of(lane * slots, slots), slots), :] = total

    @pl.when(lane == pl.num_programs(0) - 1)
    def _():
        for d in range(2):
            flipped = acc_ref[d].T
            out_ref[:, d] = flipped.reshape(out_ref.shape[0], out_ref.shape[2], out_ref.shape[3])


def correlate(got, slot_of, wins, rec_count):
    lanes = wins.shape[0]
    pairs = slot_of.shape[0]
    slots = pairs // lanes
    blocks = got.shape[3]
    lag_dev = LAGS // rec_count

    grid_spec = pltpu.PrefetchScalarGridSpec(
        num_scalar_prefetch=1,
        grid=(lanes,),
        in_specs=[
            pl.BlockSpec(got.shape, lambda l, slot: (0, 0, 0, 0)),
            pl.BlockSpec((1, 2, blocks, WIDE), lambda l, slot: (l, 0, 0, 0)),
        ],
        out_specs=pl.BlockSpec((rec_count, 2, lag_dev, pairs), lambda l, slot: (0, 0, 0, 0)),
        scratch_shapes=[
            pltpu.VMEM((2, pairs, LAGS), jnp.float32),
        ],
    )
    return pl.pallas_call(
        functools.partial(lane_kernel, slots),
        grid_spec=grid_spec,
        out_shape=jax.ShapeDtypeStruct((rec_count, 2, lag_dev, pairs), jnp.float32),
    )(slot_of, got, wins)


def per_device(waveforms, patterns, partners, counts):
    lane_dev, time_dev = waveforms.shape
    slots = partners.shape[1]
    lane_count = lax.axis_size("lane")
    rec_count = lax.axis_size("rec")
    capacity = lane_dev * slots // lane_count
    total_time = time_dev * rec_count
    blocks = time_dev // PHASE
    levels = (2 * patterns - 3).astype(jnp.bfloat16)
    prev_rim = passed_along(levels[:, time_dev - LAGS :], "rec", 1)
    next_rim = passed_along(waveforms[:, :LAGS], "rec", -1)
    span = (blocks + WIDE // PHASE) * PHASE
    wav_ext = jnp.concatenate(
        [waveforms, next_rim, jnp.zeros((lane_dev, span - time_dev - LAGS), jnp.bfloat16)], axis=1
    )
    lev_ext = jnp.concatenate(
        [prev_rim[:, 1:], levels, jnp.zeros((lane_dev, span - time_dev - LAGS + 1), jnp.bfloat16)],
        axis=1,
    )
    phased = deinterleave(jnp.stack([wav_ext, lev_ext], axis=1))
    phased = jnp.concatenate([phased[:, :1], phased[:, 1:, ::-1]], axis=1)
    phased = jnp.pad(phased, ((0, 0), (0, 0), (0, 0), (0, WIDE - phased.shape[3])))

    targets = partners.reshape(-1)
    slot_of, order = request_layout(targets, lane_dev, capacity)
    local_index = targets % lane_dev
    send_index = local_index[order].reshape(lane_count, capacity)
    index_in = lax.all_to_all(send_index, "lane", split_axis=0, concat_axis=0, tiled=True)
    both = deinterleave(jnp.stack([waveforms, levels], axis=1))
    both = jnp.concatenate([both[:, :1], both[:, 1:, ::-1]], axis=1)
    pick = (index_in.reshape(-1)[:, None] == jnp.arange(lane_dev)[None, :]).astype(jnp.bfloat16)
    reply = pick_rows(pick, both).reshape((lane_count, capacity) + both.shape[1:])
    got = lax.all_to_all(reply, "lane", split_axis=0, concat_axis=0, tiled=True)
    got = got.reshape((lane_count * capacity,) + both.shape[1:])
    lag_dev = LAGS // rec_count
    terms = correlate(got, slot_of, windows(phased, blocks), rec_count)
    parts = lax.all_to_all(terms, "rec", split_axis=0, concat_axis=0, tiled=True)
    summed = jnp.sum(parts.reshape(rec_count, 2, lag_dev, lane_dev * slots), axis=0)
    valid = (
        (jnp.arange(slots, dtype=jnp.int32)[None, :] < counts[:, None])
        .astype(jnp.float32)
        .reshape(-1)
    )
    scale = (5.0 * total_time) ** (-0.5)
    return summed * valid * scale


def solution(mesh):
    in_specs = (P("lane", "rec"), P("lane", "rec"), P("lane", None), P("lane"))
    out_specs = P(None, "rec", "lane")
    return jax.shard_map(
        per_device, mesh=mesh, in_specs=in_specs, out_specs=out_specs, check_vma=False
    )
```

```python
import math
import functools

import jax
import jax.numpy as jnp
from jax import lax
from jax.experimental import pallas as pl
from jax.experimental.pallas import tpu as pltpu
from jax.sharding import PartitionSpec as P

LAGS = 256
PHASE = 16
WIDE = 384


def passed_along(block, axis, distance):
    devices = range(lax.axis_size(axis))
    route = [(i - distance, i) for i in devices if i - distance in devices]
    return lax.ppermute(block, axis, route)


def request_layout(targets, lane_dev, capacity):
    target_dev = targets // lane_dev
    serial = jnp.arange(targets.shape[0], dtype=jnp.int32)
    earlier = (target_dev[None, :] == target_dev[:, None]) & (serial[None, :] < serial[:, None])
    ranks = jnp.sum(earlier.astype(jnp.int32), axis=1)
    slot_of = target_dev * capacity + ranks
    order = jnp.sum(jnp.where(slot_of[None, :] == serial[:, None], serial[None, :], 0), axis=1)
    return (slot_of, order)


def deinterleave(rows):
    lead = rows.shape[:-1]
    n = rows.shape[-1]
    split = rows.reshape(lead + (n // PHASE, PHASE))
    return jnp.swapaxes(split, -1, -2)


def pick_rows(onehot, table):
    flat = table.reshape(table.shape[0], -1)
    out = jnp.dot(onehot, flat, preferred_element_type=jnp.float32).astype(table.dtype)
    return out.reshape((onehot.shape[0],) + table.shape[1:])


def window_kernel(phased_ref, win_ref):
    blocks = win_ref.shape[2]
    top = WIDE // PHASE - 1
    for d in range(2):
        phased = phased_ref[0, d].astype(jnp.float32)
        parts = []
        for q in range(WIDE // PHASE):
            step = q if d == 0 else top - q
            shifted = phased if step == 0 else pltpu.roll(phased, WIDE - step, 1)
            parts.append(shifted[:, :blocks])
        win_ref[0, d] = jnp.concatenate(parts, axis=0).T.astype(jnp.bfloat16)


def windows(phased, blocks):
    lanes = phased.shape[0]
    return pl.pallas_call(
        window_kernel,
        grid=(lanes,),
        in_specs=[pl.BlockSpec((1, 2, PHASE, WIDE), lambda l: (l, 0, 0, 0))],
        out_specs=pl.BlockSpec((1, 2, blocks, WIDE), lambda l: (l, 0, 0, 0)),
        out_shape=jax.ShapeDtypeStruct((lanes, 2, blocks, WIDE), jnp.bfloat16),
    )(phased)


def lane_kernel(slots, group, slot_ref, got_ref, win_ref, out_ref, acc_ref):
    step_id = pl.program_id(0)
    for g in range(group):
        lane = step_id * group + g
        for d in range(2):
            lhs = jnp.concatenate(
                [got_ref[slot_ref[lane * slots + s], 1 - d] for s in range(slots)], axis=0
            )
            cross = lax.dot_general(
                lhs, win_ref[g, d], (((1,), (0,)), ((), ())), preferred_element_type=jnp.float32
            )
            base = WIDE - (PHASE - 1) if d == 0 else LAGS
            sums = []
            for s in range(slots):
                block = cross[s * PHASE : (s + 1) * PHASE, :]
                lined = pltpu.roll(block, base, 1, stride=1, stride_axis=0)
                sums.append(jnp.sum(lined, axis=0, keepdims=True))
            total = jnp.concatenate(sums, axis=0)[:, :LAGS]
            acc_ref[d, pl.ds(pl.multiple_of(lane * slots, slots), slots), :] = total

    @pl.when(step_id == pl.num_programs(0) - 1)
    def _():
        for d in range(2):
            flipped = acc_ref[d].T
            out_ref[:, d] = flipped.reshape(out_ref.shape[0], out_ref.shape[2], out_ref.shape[3])


def correlate(got, slot_of, wins, rec_count):
    lanes = wins.shape[0]
    pairs = slot_of.shape[0]
    slots = pairs // lanes
    blocks = got.shape[3]
    lag_dev = LAGS // rec_count
    group = math.gcd(lanes, 4)

    grid_spec = pltpu.PrefetchScalarGridSpec(
        num_scalar_prefetch=1,
        grid=(lanes // group,),
        in_specs=[
            pl.BlockSpec(got.shape, lambda l, slot: (0, 0, 0, 0)),
            pl.BlockSpec((group, 2, blocks, WIDE), lambda l, slot: (l, 0, 0, 0)),
        ],
        out_specs=pl.BlockSpec((rec_count, 2, lag_dev, pairs), lambda l, slot: (0, 0, 0, 0)),
        scratch_shapes=[
            pltpu.VMEM((2, pairs, LAGS), jnp.float32),
        ],
    )
    return pl.pallas_call(
        functools.partial(lane_kernel, slots, group),
        grid_spec=grid_spec,
        out_shape=jax.ShapeDtypeStruct((rec_count, 2, lag_dev, pairs), jnp.float32),
    )(slot_of, got, wins)


def per_device(waveforms, patterns, partners, counts):
    lane_dev, time_dev = waveforms.shape
    slots = partners.shape[1]
    lane_count = lax.axis_size("lane")
    rec_count = lax.axis_size("rec")
    capacity = lane_dev * slots // lane_count
    total_time = time_dev * rec_count
    blocks = time_dev // PHASE
    levels = (2 * patterns - 3).astype(jnp.bfloat16)
    prev_rim = passed_along(levels[:, time_dev - LAGS :], "rec", 1)
    next_rim = passed_along(waveforms[:, :LAGS], "rec", -1)
    span = (blocks + WIDE // PHASE) * PHASE
    wav_ext = jnp.concatenate(
        [waveforms, next_rim, jnp.zeros((lane_dev, span - time_dev - LAGS), jnp.bfloat16)], axis=1
    )
    lev_ext = jnp.concatenate(
        [prev_rim[:, 1:], levels, jnp.zeros((lane_dev, span - time_dev - LAGS + 1), jnp.bfloat16)],
        axis=1,
    )
    phased = deinterleave(jnp.stack([wav_ext, lev_ext], axis=1))
    phased = jnp.concatenate([phased[:, :1], phased[:, 1:, ::-1]], axis=1)
    phased = jnp.pad(phased, ((0, 0), (0, 0), (0, 0), (0, WIDE - phased.shape[3])))

    targets = partners.reshape(-1)
    slot_of, order = request_layout(targets, lane_dev, capacity)
    local_index = targets % lane_dev
    send_index = local_index[order].reshape(lane_count, capacity)
    index_in = lax.all_to_all(send_index, "lane", split_axis=0, concat_axis=0, tiled=True)
    both = deinterleave(jnp.stack([waveforms, levels], axis=1))
    both = jnp.concatenate([both[:, :1], both[:, 1:, ::-1]], axis=1)
    pick = (index_in.reshape(-1)[:, None] == jnp.arange(lane_dev)[None, :]).astype(jnp.bfloat16)
    reply = pick_rows(pick, both).reshape((lane_count, capacity) + both.shape[1:])
    got = lax.all_to_all(reply, "lane", split_axis=0, concat_axis=0, tiled=True)
    got = got.reshape((lane_count * capacity,) + both.shape[1:])
    lag_dev = LAGS // rec_count
    terms = correlate(got, slot_of, windows(phased, blocks), rec_count)
    parts = lax.all_to_all(terms, "rec", split_axis=0, concat_axis=0, tiled=True)
    summed = jnp.sum(parts.reshape(rec_count, 2, lag_dev, lane_dev * slots), axis=0)
    valid = (
        (jnp.arange(slots, dtype=jnp.int32)[None, :] < counts[:, None])
        .astype(jnp.float32)
        .reshape(-1)
    )
    scale = (5.0 * total_time) ** (-0.5)
    return summed * valid * scale


def solution(mesh):
    in_specs = (P("lane", "rec"), P("lane", "rec"), P("lane", None), P("lane"))
    out_specs = P(None, "rec", "lane")
    return jax.shard_map(
        per_device, mesh=mesh, in_specs=in_specs, out_specs=out_specs, check_vma=False
    )
```

```python
import math
import functools

import jax
import jax.numpy as jnp
from jax import lax
from jax.experimental import pallas as pl
from jax.experimental.pallas import tpu as pltpu
from jax.sharding import PartitionSpec as P

LAGS = 256
PHASE = 16
WIDE = 384


def passed_along(block, axis, distance):
    devices = range(lax.axis_size(axis))
    route = [(i - distance, i) for i in devices if i - distance in devices]
    return lax.ppermute(block, axis, route)


def request_layout(targets, lane_dev, capacity):
    target_dev = targets // lane_dev
    serial = jnp.arange(targets.shape[0], dtype=jnp.int32)
    earlier = (target_dev[None, :] == target_dev[:, None]) & (serial[None, :] < serial[:, None])
    ranks = jnp.sum(earlier.astype(jnp.int32), axis=1)
    slot_of = target_dev * capacity + ranks
    order = jnp.sum(jnp.where(slot_of[None, :] == serial[:, None], serial[None, :], 0), axis=1)
    return (slot_of, order)


def deinterleave(rows):
    lead = rows.shape[:-1]
    n = rows.shape[-1]
    split = rows.reshape(lead + (n // PHASE, PHASE))
    return jnp.swapaxes(split, -1, -2)


def pick_kernel(index_ref, table_ref, out_ref):
    def body(r, carry):
        out_ref[r] = table_ref[index_ref[r]]
        return carry

    lax.fori_loop(0, out_ref.shape[0], body, 0)


def pick_rows(index, table):
    rest = table.shape[1:]
    zeros = (0,) * len(table.shape)
    grid_spec = pltpu.PrefetchScalarGridSpec(
        num_scalar_prefetch=1,
        grid=(1,),
        in_specs=[pl.BlockSpec(table.shape, lambda g, idx: zeros)],
        out_specs=pl.BlockSpec((index.shape[0],) + rest, lambda g, idx: zeros),
    )
    return pl.pallas_call(
        pick_kernel,
        grid_spec=grid_spec,
        out_shape=jax.ShapeDtypeStruct((index.shape[0],) + rest, table.dtype),
    )(index, table)


def window_kernel(phased_ref, win_ref):
    blocks = win_ref.shape[2]
    top = WIDE // PHASE - 1
    for d in range(2):
        phased = phased_ref[0, d].astype(jnp.float32)
        parts = []
        for q in range(WIDE // PHASE):
            step = q if d == 0 else top - q
            shifted = phased if step == 0 else pltpu.roll(phased, WIDE - step, 1)
            parts.append(shifted[:, :blocks])
        win_ref[0, d] = jnp.concatenate(parts, axis=0).T.astype(jnp.bfloat16)


def windows(phased, blocks):
    lanes = phased.shape[0]
    return pl.pallas_call(
        window_kernel,
        grid=(lanes,),
        in_specs=[pl.BlockSpec((1, 2, PHASE, WIDE), lambda l: (l, 0, 0, 0))],
        out_specs=pl.BlockSpec((1, 2, blocks, WIDE), lambda l: (l, 0, 0, 0)),
        out_shape=jax.ShapeDtypeStruct((lanes, 2, blocks, WIDE), jnp.bfloat16),
    )(phased)


def lane_kernel(slots, group, slot_ref, got_ref, win_ref, out_ref, acc_ref):
    step_id = pl.program_id(0)
    for g in range(group):
        lane = step_id * group + g
        for d in range(2):
            lhs = jnp.concatenate(
                [got_ref[slot_ref[lane * slots + s], 1 - d] for s in range(slots)], axis=0
            )
            cross = lax.dot_general(
                lhs, win_ref[g, d], (((1,), (0,)), ((), ())), preferred_element_type=jnp.float32
            )
            base = WIDE - (PHASE - 1) if d == 0 else LAGS
            sums = []
            for s in range(slots):
                block = cross[s * PHASE : (s + 1) * PHASE, :]
                lined = pltpu.roll(block, base, 1, stride=1, stride_axis=0)
                sums.append(jnp.sum(lined, axis=0, keepdims=True))
            total = jnp.concatenate(sums, axis=0)[:, :LAGS]
            acc_ref[d, pl.ds(pl.multiple_of(lane * slots, slots), slots), :] = total

    @pl.when(step_id == pl.num_programs(0) - 1)
    def _():
        for d in range(2):
            flipped = acc_ref[d].T
            out_ref[:, d] = flipped.reshape(out_ref.shape[0], out_ref.shape[2], out_ref.shape[3])


def correlate(got, slot_of, wins, rec_count):
    lanes = wins.shape[0]
    pairs = slot_of.shape[0]
    slots = pairs // lanes
    blocks = got.shape[3]
    lag_dev = LAGS // rec_count
    group = math.gcd(lanes, 4)

    grid_spec = pltpu.PrefetchScalarGridSpec(
        num_scalar_prefetch=1,
        grid=(lanes // group,),
        in_specs=[
            pl.BlockSpec(got.shape, lambda l, slot: (0, 0, 0, 0)),
            pl.BlockSpec((group, 2, blocks, WIDE), lambda l, slot: (l, 0, 0, 0)),
        ],
        out_specs=pl.BlockSpec((rec_count, 2, lag_dev, pairs), lambda l, slot: (0, 0, 0, 0)),
        scratch_shapes=[
            pltpu.VMEM((2, pairs, LAGS), jnp.float32),
        ],
    )
    return pl.pallas_call(
        functools.partial(lane_kernel, slots, group),
        grid_spec=grid_spec,
        out_shape=jax.ShapeDtypeStruct((rec_count, 2, lag_dev, pairs), jnp.float32),
    )(slot_of, got, wins)


def per_device(waveforms, patterns, partners, counts):
    lane_dev, time_dev = waveforms.shape
    slots = partners.shape[1]
    lane_count = lax.axis_size("lane")
    rec_count = lax.axis_size("rec")
    capacity = lane_dev * slots // lane_count
    total_time = time_dev * rec_count
    blocks = time_dev // PHASE
    levels = (2 * patterns - 3).astype(jnp.bfloat16)
    prev_rim = passed_along(levels[:, time_dev - LAGS :], "rec", 1)
    next_rim = passed_along(waveforms[:, :LAGS], "rec", -1)
    span = (blocks + WIDE // PHASE) * PHASE
    wav_ext = jnp.concatenate(
        [waveforms, next_rim, jnp.zeros((lane_dev, span - time_dev - LAGS), jnp.bfloat16)], axis=1
    )
    lev_ext = jnp.concatenate(
        [prev_rim[:, 1:], levels, jnp.zeros((lane_dev, span - time_dev - LAGS + 1), jnp.bfloat16)],
        axis=1,
    )
    phased = deinterleave(jnp.stack([wav_ext, lev_ext], axis=1))
    phased = jnp.concatenate([phased[:, :1], phased[:, 1:, ::-1]], axis=1)
    phased = jnp.pad(phased, ((0, 0), (0, 0), (0, 0), (0, WIDE - phased.shape[3])))

    targets = partners.reshape(-1)
    slot_of, order = request_layout(targets, lane_dev, capacity)
    local_index = targets % lane_dev
    send_index = local_index[order].reshape(lane_count, capacity)
    index_in = lax.all_to_all(send_index, "lane", split_axis=0, concat_axis=0, tiled=True)
    both = deinterleave(jnp.stack([waveforms, levels], axis=1))
    both = jnp.concatenate([both[:, :1], both[:, 1:, ::-1]], axis=1)
    reply = pick_rows(index_in.reshape(-1), both).reshape((lane_count, capacity) + both.shape[1:])
    got = lax.all_to_all(reply, "lane", split_axis=0, concat_axis=0, tiled=True)
    got = got.reshape((lane_count * capacity,) + both.shape[1:])
    lag_dev = LAGS // rec_count
    terms = correlate(got, slot_of, windows(phased, blocks), rec_count)
    parts = lax.all_to_all(terms, "rec", split_axis=0, concat_axis=0, tiled=True)
    summed = jnp.sum(parts.reshape(rec_count, 2, lag_dev, lane_dev * slots), axis=0)
    valid = (
        (jnp.arange(slots, dtype=jnp.int32)[None, :] < counts[:, None])
        .astype(jnp.float32)
        .reshape(-1)
    )
    scale = (5.0 * total_time) ** (-0.5)
    return summed * valid * scale


def solution(mesh):
    in_specs = (P("lane", "rec"), P("lane", "rec"), P("lane", None), P("lane"))
    out_specs = P(None, "rec", "lane")
    return jax.shard_map(
        per_device, mesh=mesh, in_specs=in_specs, out_specs=out_specs, check_vma=False
    )
```

```python
import math
import functools

import jax
import jax.numpy as jnp
from jax import lax
from jax.experimental import pallas as pl
from jax.experimental.pallas import tpu as pltpu
from jax.sharding import PartitionSpec as P

LAGS = 256
PHASE = 16
WIDE = 384


def passed_along(block, axis, distance):
    devices = range(lax.axis_size(axis))
    route = [(i - distance, i) for i in devices if i - distance in devices]
    return lax.ppermute(block, axis, route)


def request_layout(targets, lane_dev, capacity):
    target_dev = targets // lane_dev
    serial = jnp.arange(targets.shape[0], dtype=jnp.int32)
    earlier = (target_dev[None, :] == target_dev[:, None]) & (serial[None, :] < serial[:, None])
    ranks = jnp.sum(earlier.astype(jnp.int32), axis=1)
    slot_of = target_dev * capacity + ranks
    order = jnp.sum(jnp.where(slot_of[None, :] == serial[:, None], serial[None, :], 0), axis=1)
    return (slot_of, order)


def deinterleave(rows):
    lead = rows.shape[:-1]
    n = rows.shape[-1]
    split = rows.reshape(lead + (n // PHASE, PHASE))
    return jnp.swapaxes(split, -1, -2)


def pick_rows(onehot, table):
    flat = table.reshape(table.shape[0], -1)
    out = jnp.dot(onehot, flat, preferred_element_type=jnp.float32).astype(table.dtype)
    return out.reshape((onehot.shape[0],) + table.shape[1:])


def window_kernel(phased_ref, win_ref):
    blocks = win_ref.shape[2]
    top = WIDE // PHASE - 1
    for d in range(2):
        phased = phased_ref[0, d].astype(jnp.float32)
        parts = []
        for q in range(WIDE // PHASE):
            step = q if d == 0 else top - q
            shifted = phased if step == 0 else pltpu.roll(phased, WIDE - step, 1)
            parts.append(shifted[:, :blocks])
        win_ref[0, d] = jnp.concatenate(parts, axis=0).T.astype(jnp.bfloat16)


def windows(phased, blocks):
    lanes = phased.shape[0]
    return pl.pallas_call(
        window_kernel,
        grid=(lanes,),
        in_specs=[pl.BlockSpec((1, 2, PHASE, WIDE), lambda l: (l, 0, 0, 0))],
        out_specs=pl.BlockSpec((1, 2, blocks, WIDE), lambda l: (l, 0, 0, 0)),
        out_shape=jax.ShapeDtypeStruct((lanes, 2, blocks, WIDE), jnp.bfloat16),
    )(phased)


def lane_kernel(slots, group, slot_ref, got_ref, win_ref, out_ref, acc_ref):
    step_id = pl.program_id(0)
    for g in range(group):
        lane = step_id * group + g
        for d in range(2):
            lhs = jnp.concatenate(
                [got_ref[slot_ref[lane * slots + s], 1 - d] for s in range(slots)], axis=0
            )
            cross = lax.dot_general(
                lhs, win_ref[g, d], (((1,), (0,)), ((), ())), preferred_element_type=jnp.float32
            )
            base = WIDE - (PHASE - 1) if d == 0 else LAGS
            sums = []
            for s in range(slots):
                block = cross[s * PHASE : (s + 1) * PHASE, :]
                lined = pltpu.roll(block, base, 1, stride=1, stride_axis=0)
                sums.append(jnp.sum(lined, axis=0, keepdims=True))
            total = jnp.concatenate(sums, axis=0)[:, :LAGS]
            acc_ref[d, pl.ds(pl.multiple_of(lane * slots, slots), slots), :] = total

    @pl.when(step_id == pl.num_programs(0) - 1)
    def _():
        for d in range(2):
            flipped = acc_ref[d].T
            out_ref[:, d] = flipped.reshape(out_ref.shape[0], out_ref.shape[2], out_ref.shape[3])


def correlate(got, slot_of, wins, rec_count):
    lanes = wins.shape[0]
    pairs = slot_of.shape[0]
    slots = pairs // lanes
    blocks = got.shape[3]
    lag_dev = LAGS // rec_count
    group = math.gcd(lanes, 8)

    grid_spec = pltpu.PrefetchScalarGridSpec(
        num_scalar_prefetch=1,
        grid=(lanes // group,),
        in_specs=[
            pl.BlockSpec(got.shape, lambda l, slot: (0, 0, 0, 0)),
            pl.BlockSpec((group, 2, blocks, WIDE), lambda l, slot: (l, 0, 0, 0)),
        ],
        out_specs=pl.BlockSpec((rec_count, 2, lag_dev, pairs), lambda l, slot: (0, 0, 0, 0)),
        scratch_shapes=[
            pltpu.VMEM((2, pairs, LAGS), jnp.float32),
        ],
    )
    return pl.pallas_call(
        functools.partial(lane_kernel, slots, group),
        grid_spec=grid_spec,
        out_shape=jax.ShapeDtypeStruct((rec_count, 2, lag_dev, pairs), jnp.float32),
    )(slot_of, got, wins)


def per_device(waveforms, patterns, partners, counts):
    lane_dev, time_dev = waveforms.shape
    slots = partners.shape[1]
    lane_count = lax.axis_size("lane")
    rec_count = lax.axis_size("rec")
    capacity = lane_dev * slots // lane_count
    total_time = time_dev * rec_count
    blocks = time_dev // PHASE
    levels = (2 * patterns - 3).astype(jnp.bfloat16)
    prev_rim = passed_along(levels[:, time_dev - LAGS :], "rec", 1)
    next_rim = passed_along(waveforms[:, :LAGS], "rec", -1)
    span = (blocks + WIDE // PHASE) * PHASE
    wav_ext = jnp.concatenate(
        [waveforms, next_rim, jnp.zeros((lane_dev, span - time_dev - LAGS), jnp.bfloat16)], axis=1
    )
    lev_ext = jnp.concatenate(
        [prev_rim[:, 1:], levels, jnp.zeros((lane_dev, span - time_dev - LAGS + 1), jnp.bfloat16)],
        axis=1,
    )
    phased = deinterleave(jnp.stack([wav_ext, lev_ext], axis=1))
    phased = jnp.concatenate([phased[:, :1], phased[:, 1:, ::-1]], axis=1)
    phased = jnp.pad(phased, ((0, 0), (0, 0), (0, 0), (0, WIDE - phased.shape[3])))

    targets = partners.reshape(-1)
    slot_of, order = request_layout(targets, lane_dev, capacity)
    local_index = targets % lane_dev
    send_index = local_index[order].reshape(lane_count, capacity)
    index_in = lax.all_to_all(send_index, "lane", split_axis=0, concat_axis=0, tiled=True)
    both = deinterleave(jnp.stack([waveforms, levels], axis=1))
    both = jnp.concatenate([both[:, :1], both[:, 1:, ::-1]], axis=1)
    pick = (index_in.reshape(-1)[:, None] == jnp.arange(lane_dev)[None, :]).astype(jnp.bfloat16)
    reply = pick_rows(pick, both).reshape((lane_count, capacity) + both.shape[1:])
    got = lax.all_to_all(reply, "lane", split_axis=0, concat_axis=0, tiled=True)
    got = got.reshape((lane_count * capacity,) + both.shape[1:])
    lag_dev = LAGS // rec_count
    terms = correlate(got, slot_of, windows(phased, blocks), rec_count)
    parts = lax.all_to_all(terms, "rec", split_axis=0, concat_axis=0, tiled=True)
    summed = jnp.sum(parts.reshape(rec_count, 2, lag_dev, lane_dev * slots), axis=0)
    valid = (
        (jnp.arange(slots, dtype=jnp.int32)[None, :] < counts[:, None])
        .astype(jnp.float32)
        .reshape(-1)
    )
    scale = (5.0 * total_time) ** (-0.5)
    return summed * valid * scale


def solution(mesh):
    in_specs = (P("lane", "rec"), P("lane", "rec"), P("lane", None), P("lane"))
    out_specs = P(None, "rec", "lane")
    return jax.shard_map(
        per_device, mesh=mesh, in_specs=in_specs, out_specs=out_specs, check_vma=False
    )
```

```python
import math
import functools

import jax
import jax.numpy as jnp
from jax import lax
from jax.experimental import pallas as pl
from jax.experimental.pallas import tpu as pltpu
from jax.sharding import PartitionSpec as P

LAGS = 256
PHASE = 16
WIDE = 384


def passed_along(block, axis, distance):
    devices = range(lax.axis_size(axis))
    route = [(i - distance, i) for i in devices if i - distance in devices]
    return lax.ppermute(block, axis, route)


def request_layout(targets, lane_dev, capacity):
    target_dev = targets // lane_dev
    serial = jnp.arange(targets.shape[0], dtype=jnp.int32)
    earlier = (target_dev[None, :] == target_dev[:, None]) & (serial[None, :] < serial[:, None])
    ranks = jnp.sum(earlier.astype(jnp.int32), axis=1)
    slot_of = target_dev * capacity + ranks
    order = jnp.sum(jnp.where(slot_of[None, :] == serial[:, None], serial[None, :], 0), axis=1)
    return (slot_of, order)


def deinterleave(rows):
    lead = rows.shape[:-1]
    n = rows.shape[-1]
    split = rows.reshape(lead + (n // PHASE, PHASE))
    return jnp.swapaxes(split, -1, -2)


def window_kernel(phased_ref, win_ref):
    blocks = win_ref.shape[2]
    top = WIDE // PHASE - 1
    for d in range(2):
        phased = phased_ref[0, d].astype(jnp.float32)
        parts = []
        for q in range(WIDE // PHASE):
            step = q if d == 0 else top - q
            shifted = phased if step == 0 else pltpu.roll(phased, WIDE - step, 1)
            parts.append(shifted[:, :blocks])
        win_ref[0, d] = jnp.concatenate(parts, axis=0).T.astype(jnp.bfloat16)


def windows(phased, blocks):
    lanes = phased.shape[0]
    return pl.pallas_call(
        window_kernel,
        grid=(lanes,),
        in_specs=[pl.BlockSpec((1, 2, PHASE, WIDE), lambda l: (l, 0, 0, 0))],
        out_specs=pl.BlockSpec((1, 2, blocks, WIDE), lambda l: (l, 0, 0, 0)),
        out_shape=jax.ShapeDtypeStruct((lanes, 2, blocks, WIDE), jnp.bfloat16),
    )(phased)


def lane_kernel(slots, group, slot_ref, got_ref, win_ref, out_ref, acc_ref):
    step_id = pl.program_id(0)
    for g in range(group):
        lane = step_id * group + g
        for d in range(2):
            lhs = jnp.concatenate(
                [got_ref[slot_ref[lane * slots + s], 1 - d] for s in range(slots)], axis=0
            )
            cross = lax.dot_general(
                lhs, win_ref[g, d], (((1,), (0,)), ((), ())), preferred_element_type=jnp.float32
            )
            base = WIDE - (PHASE - 1) if d == 0 else LAGS
            sums = []
            for s in range(slots):
                block = cross[s * PHASE : (s + 1) * PHASE, :]
                lined = pltpu.roll(block, base, 1, stride=1, stride_axis=0)
                sums.append(jnp.sum(lined, axis=0, keepdims=True))
            total = jnp.concatenate(sums, axis=0)[:, :LAGS]
            acc_ref[d, pl.ds(pl.multiple_of(lane * slots, slots), slots), :] = total

    @pl.when(step_id == pl.num_programs(0) - 1)
    def _():
        for d in range(2):
            flipped = acc_ref[d].T
            out_ref[:, d] = flipped.reshape(out_ref.shape[0], out_ref.shape[2], out_ref.shape[3])


def correlate(got, slot_of, wins, rec_count):
    lanes = wins.shape[0]
    pairs = slot_of.shape[0]
    slots = pairs // lanes
    blocks = got.shape[3]
    lag_dev = LAGS // rec_count
    group = math.gcd(lanes, 8)

    grid_spec = pltpu.PrefetchScalarGridSpec(
        num_scalar_prefetch=1,
        grid=(lanes // group,),
        in_specs=[
            pl.BlockSpec(got.shape, lambda l, slot: (0, 0, 0, 0)),
            pl.BlockSpec((group, 2, blocks, WIDE), lambda l, slot: (l, 0, 0, 0)),
        ],
        out_specs=pl.BlockSpec((rec_count, 2, lag_dev, pairs), lambda l, slot: (0, 0, 0, 0)),
        scratch_shapes=[
            pltpu.VMEM((2, pairs, LAGS), jnp.float32),
        ],
    )
    return pl.pallas_call(
        functools.partial(lane_kernel, slots, group),
        grid_spec=grid_spec,
        out_shape=jax.ShapeDtypeStruct((rec_count, 2, lag_dev, pairs), jnp.float32),
    )(slot_of, got, wins)


def per_device(waveforms, patterns, partners, counts):
    lane_dev, time_dev = waveforms.shape
    slots = partners.shape[1]
    lane_count = lax.axis_size("lane")
    rec_count = lax.axis_size("rec")
    capacity = lane_dev * slots // lane_count
    total_time = time_dev * rec_count
    blocks = time_dev // PHASE
    levels = (2 * patterns - 3).astype(jnp.bfloat16)
    prev_rim = passed_along(levels[:, time_dev - LAGS :], "rec", 1)
    next_rim = passed_along(waveforms[:, :LAGS], "rec", -1)
    span = (blocks + WIDE // PHASE) * PHASE
    wav_ext = jnp.concatenate(
        [waveforms, next_rim, jnp.zeros((lane_dev, span - time_dev - LAGS), jnp.bfloat16)], axis=1
    )
    lev_ext = jnp.concatenate(
        [prev_rim[:, 1:], levels, jnp.zeros((lane_dev, span - time_dev - LAGS + 1), jnp.bfloat16)],
        axis=1,
    )
    phased = deinterleave(jnp.stack([wav_ext, lev_ext], axis=1))
    phased = jnp.concatenate([phased[:, :1], phased[:, 1:, ::-1]], axis=1)
    phased = jnp.pad(phased, ((0, 0), (0, 0), (0, 0), (0, WIDE - phased.shape[3])))

    targets = partners.reshape(-1)
    slot_of, order = request_layout(targets, lane_dev, capacity)
    local_index = targets % lane_dev
    send_index = local_index[order].reshape(lane_count, capacity)
    index_in = lax.all_to_all(send_index, "lane", split_axis=0, concat_axis=0, tiled=True)
    both = deinterleave(jnp.stack([waveforms, levels], axis=1))
    both = jnp.concatenate([both[:, :1], both[:, 1:, ::-1]], axis=1)
    reply = both[index_in.reshape(-1)].reshape((lane_count, capacity) + both.shape[1:])
    got = lax.all_to_all(reply, "lane", split_axis=0, concat_axis=0, tiled=True)
    got = got.reshape((lane_count * capacity,) + both.shape[1:])
    lag_dev = LAGS // rec_count
    terms = correlate(got, slot_of, windows(phased, blocks), rec_count)
    parts = lax.all_to_all(terms, "rec", split_axis=0, concat_axis=0, tiled=True)
    summed = jnp.sum(parts.reshape(rec_count, 2, lag_dev, lane_dev * slots), axis=0)
    valid = (
        (jnp.arange(slots, dtype=jnp.int32)[None, :] < counts[:, None])
        .astype(jnp.float32)
        .reshape(-1)
    )
    scale = (5.0 * total_time) ** (-0.5)
    return summed * valid * scale


def solution(mesh):
    in_specs = (P("lane", "rec"), P("lane", "rec"), P("lane", None), P("lane"))
    out_specs = P(None, "rec", "lane")
    return jax.shard_map(
        per_device, mesh=mesh, in_specs=in_specs, out_specs=out_specs, check_vma=False
    )
```

```python
import math
import functools

import jax
import jax.numpy as jnp
from jax import lax
from jax.experimental import pallas as pl
from jax.experimental.pallas import tpu as pltpu
from jax.sharding import PartitionSpec as P

LAGS = 256
PHASE = 16
WIDE = 384


def passed_along(block, axis, distance):
    devices = range(lax.axis_size(axis))
    route = [(i - distance, i) for i in devices if i - distance in devices]
    return lax.ppermute(block, axis, route)


def request_layout(targets, lane_dev, capacity):
    target_dev = targets // lane_dev
    serial = jnp.arange(targets.shape[0], dtype=jnp.int32)
    earlier = (target_dev[None, :] == target_dev[:, None]) & (serial[None, :] < serial[:, None])
    ranks = jnp.sum(earlier.astype(jnp.int32), axis=1)
    slot_of = target_dev * capacity + ranks
    order = jnp.sum(jnp.where(slot_of[None, :] == serial[:, None], serial[None, :], 0), axis=1)
    return (slot_of, order)


def deinterleave(rows):
    lead = rows.shape[:-1]
    n = rows.shape[-1]
    split = rows.reshape(lead + (n // PHASE, PHASE))
    return jnp.swapaxes(split, -1, -2)


def window_kernel(phased_ref, win_ref):
    blocks = win_ref.shape[2]
    top = WIDE // PHASE - 1
    for d in range(2):
        phased = phased_ref[0, d].astype(jnp.float32)
        parts = []
        for q in range(WIDE // PHASE):
            step = q if d == 0 else top - q
            shifted = phased if step == 0 else pltpu.roll(phased, WIDE - step, 1)
            parts.append(shifted[:, :blocks])
        win_ref[0, d] = jnp.concatenate(parts, axis=0).T.astype(jnp.bfloat16)


def windows(phased, blocks):
    lanes = phased.shape[0]
    return pl.pallas_call(
        window_kernel,
        grid=(lanes,),
        in_specs=[pl.BlockSpec((1, 2, PHASE, WIDE), lambda l: (l, 0, 0, 0))],
        out_specs=pl.BlockSpec((1, 2, blocks, WIDE), lambda l: (l, 0, 0, 0)),
        out_shape=jax.ShapeDtypeStruct((lanes, 2, blocks, WIDE), jnp.bfloat16),
    )(phased)


def lane_kernel(slots, group, slot_ref, got_ref, win_ref, out_ref, acc_ref):
    step_id = pl.program_id(0)
    for g in range(group):
        lane = step_id * group + g
        for d in range(2):
            lhs = jnp.concatenate(
                [got_ref[slot_ref[lane * slots + s], 1 - d] for s in range(slots)], axis=0
            )
            cross = lax.dot_general(
                lhs, win_ref[g, d], (((1,), (0,)), ((), ())), preferred_element_type=jnp.float32
            )
            base = WIDE - (PHASE - 1) if d == 0 else LAGS
            sums = []
            for s in range(slots):
                block = cross[s * PHASE : (s + 1) * PHASE, :]
                lined = pltpu.roll(block, base, 1, stride=1, stride_axis=0)
                sums.append(jnp.sum(lined, axis=0, keepdims=True))
            total = jnp.concatenate(sums, axis=0)[:, :LAGS]
            acc_ref[d, pl.ds(pl.multiple_of(lane * slots, slots), slots), :] = total

    @pl.when(step_id == pl.num_programs(0) - 1)
    def _():
        for d in range(2):
            flipped = acc_ref[d].T
            out_ref[:, d] = flipped.reshape(out_ref.shape[0], out_ref.shape[2], out_ref.shape[3])


def correlate(got, slot_of, wins, rec_count):
    lanes = wins.shape[0]
    pairs = slot_of.shape[0]
    slots = pairs // lanes
    blocks = got.shape[3]
    lag_dev = LAGS // rec_count
    group = math.gcd(lanes, 8)

    grid_spec = pltpu.PrefetchScalarGridSpec(
        num_scalar_prefetch=1,
        grid=(lanes // group,),
        in_specs=[
            pl.BlockSpec(got.shape, lambda l, slot: (0, 0, 0, 0)),
            pl.BlockSpec((group, 2, blocks, WIDE), lambda l, slot: (l, 0, 0, 0)),
        ],
        out_specs=pl.BlockSpec((rec_count, 2, lag_dev, pairs), lambda l, slot: (0, 0, 0, 0)),
        scratch_shapes=[
            pltpu.VMEM((2, pairs, LAGS), jnp.float32),
        ],
    )
    return pl.pallas_call(
        functools.partial(lane_kernel, slots, group),
        grid_spec=grid_spec,
        out_shape=jax.ShapeDtypeStruct((rec_count, 2, lag_dev, pairs), jnp.float32),
    )(slot_of, got, wins)


def per_device(waveforms, patterns, partners, counts):
    lane_dev, time_dev = waveforms.shape
    slots = partners.shape[1]
    lane_count = lax.axis_size("lane")
    rec_count = lax.axis_size("rec")
    capacity = lane_dev * slots // lane_count
    total_time = time_dev * rec_count
    blocks = time_dev // PHASE
    levels = (2 * patterns - 3).astype(jnp.bfloat16)
    prev_rim = passed_along(levels[:, time_dev - LAGS :], "rec", 1)
    next_rim = passed_along(waveforms[:, :LAGS], "rec", -1)
    span = (blocks + WIDE // PHASE) * PHASE
    wav_ext = jnp.concatenate(
        [waveforms, next_rim, jnp.zeros((lane_dev, span - time_dev - LAGS), jnp.bfloat16)], axis=1
    )
    lev_ext = jnp.concatenate(
        [prev_rim[:, 1:], levels, jnp.zeros((lane_dev, span - time_dev - LAGS + 1), jnp.bfloat16)],
        axis=1,
    )
    phased = deinterleave(jnp.stack([wav_ext, lev_ext], axis=1))
    phased = jnp.concatenate([phased[:, :1], phased[:, 1:, ::-1]], axis=1)
    phased = jnp.pad(phased, ((0, 0), (0, 0), (0, 0), (0, WIDE - phased.shape[3])))

    targets = partners.reshape(-1)
    slot_of, _ = request_layout(targets, lane_dev, capacity)
    local_index = targets % lane_dev
    serial = jnp.arange(targets.shape[0], dtype=jnp.int32)
    chosen = slot_of[None, :] == serial[:, None]
    send_index = jnp.sum(jnp.where(chosen, local_index[None, :], 0), axis=1)
    send_index = send_index.reshape(lane_count, capacity)
    index_in = lax.all_to_all(send_index, "lane", split_axis=0, concat_axis=0, tiled=True)
    both = deinterleave(jnp.stack([waveforms, levels], axis=1))
    both = jnp.concatenate([both[:, :1], both[:, 1:, ::-1]], axis=1)
    reply = both[index_in.reshape(-1)].reshape((lane_count, capacity) + both.shape[1:])
    got = lax.all_to_all(reply, "lane", split_axis=0, concat_axis=0, tiled=True)
    got = got.reshape((lane_count * capacity,) + both.shape[1:])
    lag_dev = LAGS // rec_count
    terms = correlate(got, slot_of, windows(phased, blocks), rec_count)
    parts = lax.all_to_all(terms, "rec", split_axis=0, concat_axis=0, tiled=True)
    summed = jnp.sum(parts.reshape(rec_count, 2, lag_dev, lane_dev * slots), axis=0)
    valid = (
        (jnp.arange(slots, dtype=jnp.int32)[None, :] < counts[:, None])
        .astype(jnp.float32)
        .reshape(-1)
    )
    scale = (5.0 * total_time) ** (-0.5)
    return summed * valid * scale


def solution(mesh):
    in_specs = (P("lane", "rec"), P("lane", "rec"), P("lane", None), P("lane"))
    out_specs = P(None, "rec", "lane")
    return jax.shard_map(
        per_device, mesh=mesh, in_specs=in_specs, out_specs=out_specs, check_vma=False
    )
```

```python
import math
import functools

import jax
import jax.numpy as jnp
from jax import lax
from jax.experimental import pallas as pl
from jax.experimental.pallas import tpu as pltpu
from jax.sharding import PartitionSpec as P

LAGS = 256
PHASE = 16
WIDE = 384


def passed_along(block, axis, distance):
    devices = range(lax.axis_size(axis))
    route = [(i - distance, i) for i in devices if i - distance in devices]
    return lax.ppermute(block, axis, route)


def request_layout(targets, lane_dev, capacity):
    target_dev = targets // lane_dev
    serial = jnp.arange(targets.shape[0], dtype=jnp.int32)
    earlier = (target_dev[None, :] == target_dev[:, None]) & (serial[None, :] < serial[:, None])
    ranks = jnp.sum(earlier.astype(jnp.int32), axis=1)
    slot_of = target_dev * capacity + ranks
    order = jnp.sum(jnp.where(slot_of[None, :] == serial[:, None], serial[None, :], 0), axis=1)
    return (slot_of, order)


def deinterleave(rows):
    lead = rows.shape[:-1]
    n = rows.shape[-1]
    split = rows.reshape(lead + (n // PHASE, PHASE))
    return jnp.swapaxes(split, -1, -2)


def window_kernel(phased_ref, win_ref):
    blocks = win_ref.shape[2]
    top = WIDE // PHASE - 1
    for d in range(2):
        phased = phased_ref[0, d].astype(jnp.float32)
        parts = []
        for q in range(WIDE // PHASE):
            step = q if d == 0 else top - q
            shifted = phased if step == 0 else pltpu.roll(phased, WIDE - step, 1)
            parts.append(shifted[:, :blocks])
        win_ref[0, d] = jnp.concatenate(parts, axis=0).T.astype(jnp.bfloat16)


def windows(phased, blocks):
    lanes = phased.shape[0]
    return pl.pallas_call(
        window_kernel,
        grid=(lanes,),
        in_specs=[pl.BlockSpec((1, 2, PHASE, WIDE), lambda l: (l, 0, 0, 0))],
        out_specs=pl.BlockSpec((1, 2, blocks, WIDE), lambda l: (l, 0, 0, 0)),
        out_shape=jax.ShapeDtypeStruct((lanes, 2, blocks, WIDE), jnp.bfloat16),
    )(phased)


def lane_kernel(slots, group, slot_ref, got_ref, win_ref, out_ref, acc_ref):
    step_id = pl.program_id(0)
    for g in range(group):
        lane = step_id * group + g
        for d in range(2):
            lhs = jnp.concatenate(
                [got_ref[slot_ref[lane * slots + s], 1 - d] for s in range(slots)], axis=0
            )
            cross = lax.dot_general(
                lhs, win_ref[g, d], (((1,), (0,)), ((), ())), preferred_element_type=jnp.float32
            )
            base = WIDE - (PHASE - 1) if d == 0 else LAGS
            sums = []
            for s in range(slots):
                block = cross[s * PHASE : (s + 1) * PHASE, :]
                lined = pltpu.roll(block, base, 1, stride=1, stride_axis=0)
                sums.append(jnp.sum(lined, axis=0, keepdims=True))
            total = jnp.concatenate(sums, axis=0)[:, :LAGS]
            acc_ref[d, pl.ds(pl.multiple_of(lane * slots, slots), slots), :] = total

    @pl.when(step_id == pl.num_programs(0) - 1)
    def _():
        for d in range(2):
            flipped = acc_ref[d].T
            out_ref[:, d] = flipped.reshape(out_ref.shape[0], out_ref.shape[2], out_ref.shape[3])


def correlate(got, slot_of, wins, rec_count):
    lanes = wins.shape[0]
    pairs = slot_of.shape[0]
    slots = pairs // lanes
    blocks = got.shape[3]
    lag_dev = LAGS // rec_count
    group = math.gcd(lanes, 8)

    grid_spec = pltpu.PrefetchScalarGridSpec(
        num_scalar_prefetch=1,
        grid=(lanes // group,),
        in_specs=[
            pl.BlockSpec(got.shape, lambda l, slot: (0, 0, 0, 0)),
            pl.BlockSpec((group, 2, blocks, WIDE), lambda l, slot: (l, 0, 0, 0)),
        ],
        out_specs=pl.BlockSpec((rec_count, 2, lag_dev, pairs), lambda l, slot: (0, 0, 0, 0)),
        scratch_shapes=[
            pltpu.VMEM((2, pairs, LAGS), jnp.float32),
        ],
    )
    return pl.pallas_call(
        functools.partial(lane_kernel, slots, group),
        grid_spec=grid_spec,
        out_shape=jax.ShapeDtypeStruct((rec_count, 2, lag_dev, pairs), jnp.float32),
    )(slot_of, got, wins)


def per_device(waveforms, patterns, partners, counts):
    lane_dev, time_dev = waveforms.shape
    slots = partners.shape[1]
    lane_count = lax.axis_size("lane")
    rec_count = lax.axis_size("rec")
    capacity = lane_dev * slots // lane_count
    total_time = time_dev * rec_count
    blocks = time_dev // PHASE
    levels = (2 * patterns - 3).astype(jnp.bfloat16)
    prev_rim = passed_along(levels[:, time_dev - LAGS :], "rec", 1)
    next_rim = passed_along(waveforms[:, :LAGS], "rec", -1)
    span = (blocks + WIDE // PHASE) * PHASE
    wav_ext = jnp.concatenate(
        [waveforms, next_rim, jnp.zeros((lane_dev, span - time_dev - LAGS), jnp.bfloat16)], axis=1
    )
    lev_ext = jnp.concatenate(
        [prev_rim[:, 1:], levels, jnp.zeros((lane_dev, span - time_dev - LAGS + 1), jnp.bfloat16)],
        axis=1,
    )
    phased = deinterleave(jnp.stack([wav_ext, lev_ext], axis=1))
    phased = jnp.concatenate([phased[:, :1], phased[:, 1:, ::-1]], axis=1)
    phased = jnp.pad(phased, ((0, 0), (0, 0), (0, 0), (0, WIDE - phased.shape[3])))

    targets = partners.reshape(-1)
    slot_of, _ = request_layout(targets, lane_dev, capacity)
    local_index = targets % lane_dev
    serial = jnp.arange(targets.shape[0], dtype=jnp.int32)
    chosen = slot_of[None, :] == serial[:, None]
    send_index = jnp.sum(jnp.where(chosen, local_index[None, :], 0), axis=1)
    send_index = send_index.reshape(lane_count, capacity)
    index_in = lax.all_to_all(send_index, "lane", split_axis=0, concat_axis=0, tiled=True)
    both = deinterleave(jnp.stack([waveforms, levels], axis=1))
    both = jnp.concatenate([both[:, :1], both[:, 1:, ::-1]], axis=1)
    reply = jnp.take(both, index_in.reshape(-1), axis=0, mode="clip")
    reply = reply.reshape((lane_count, capacity) + both.shape[1:])
    got = lax.all_to_all(reply, "lane", split_axis=0, concat_axis=0, tiled=True)
    got = got.reshape((lane_count * capacity,) + both.shape[1:])
    lag_dev = LAGS // rec_count
    terms = correlate(got, slot_of, windows(phased, blocks), rec_count)
    parts = lax.all_to_all(terms, "rec", split_axis=0, concat_axis=0, tiled=True)
    summed = jnp.sum(parts.reshape(rec_count, 2, lag_dev, lane_dev * slots), axis=0)
    valid = (
        (jnp.arange(slots, dtype=jnp.int32)[None, :] < counts[:, None])
        .astype(jnp.float32)
        .reshape(-1)
    )
    scale = (5.0 * total_time) ** (-0.5)
    return summed * valid * scale


def solution(mesh):
    in_specs = (P("lane", "rec"), P("lane", "rec"), P("lane", None), P("lane"))
    out_specs = P(None, "rec", "lane")
    return jax.shard_map(
        per_device, mesh=mesh, in_specs=in_specs, out_specs=out_specs, check_vma=False
    )
```
